768 devices in a mesh: stream: 64 (over x, y, core), span: 12 (over z).
Axes of the slice: x: 4, y: 8, z: 12, core: 2. Of those that a mesh axis runs over, the one named last changes fastest.
Arguments:
- right_side: float32 [64, 12, 96, 512], P('stream', 'span'), may hold values from -11 to 11
- conductance: float32 [64, 12, 96], P('stream', 'span'), may hold values from 0.3 to 3
- element_slot: int32 [64, 12, 96], P('stream', 'span'), may hold values from 0 to 95, each once within a row
Outputs:
- solution_field: float32 [64, 12, 96, 512], P('stream', 'span')
- residual: float32 [64, 12, 96, 512], P('stream', 'span')
The draws below stay inside these ranges and needn't reach their ends.
Inputs may be any that keep to these rules, and one draw needn't show every extreme that they name: element_slot[s, p] names every slot of 0 to 95 once.
All inputs are finite; a program needn't handle non-finite values.
Results may differ from the reference program's by a relative error of at most 0.00027.
Values sent between devices are 32-bit elements; how exact they have to be, the bound alone decides.
No kernel may reach another device: no remote copies, remote signals or barrier semaphores. Data moves between devices by JAX's collectives and lax.ppermute only.
A program may use at most 64 MiB of HBM per device.

```python
import math
import jax
import jax.numpy as jnp
import numpy as np
from jax import lax

TX = 2
TY = 2
TZ = 24
NODES = 512
ITERS = 2
E_DEV = 96
NS_TILES = 64
NP_TILES = 12
N_STREAM = 64
N_SPAN = 12


def draw_right_side(key, part):
    rough_key = jax.random.fold_in(key, 11)
    level_key = jax.random.fold_in(key, 12)
    sign_key = jax.random.fold_in(key, 13)
    full_shape = (NS_TILES, NP_TILES, E_DEV, NODES)
    tile_shape = (NS_TILES, NP_TILES, 1, 1)
    level = jnp.exp(jax.random.uniform(level_key, tile_shape, jnp.float32, math.log(0.25), math.log(2.5)))
    rough = jnp.clip(jax.random.normal(rough_key, full_shape, jnp.float32), -8.0, 8.0)
    flips = jax.random.bernoulli(sign_key, 0.5, tile_shape)
    smooth = level * jnp.where(flips, 1.0, -1.0)
    return (rough + smooth).astype(jnp.float32)


def steps_of(key, shape, cuts, least, largest):
    factor_of, own = 1.0, jax.random.fold_in(key, 6)
    for position, shards_of in cuts:
        heights = jnp.exp(jax.random.uniform(jax.random.fold_in(own, position), (shards_of,), jnp.float32, least / len(cuts), largest / len(cuts)))
        factor_of = factor_of * jnp.repeat(heights, shape[position] // shards_of).reshape([-1 if axis == position else 1 for axis in range(len(shape))])
    return factor_of


def setup_inputs(seed: int = 0) -> dict:
    seeds = jax.random.split(jax.random.key(seed), 4)
    right_side = draw_right_side(jax.random.fold_in(seeds[3], 71), 0)
    conductance = jnp.clip(jnp.exp(math.log(3.0) - 2.3025851 * jax.random.uniform(seeds[1], (NS_TILES, NP_TILES, E_DEV), jnp.float32) ** steps_of(seeds[1], (NS_TILES, NP_TILES, E_DEV), ((0, 64), (1, 12)), -0.2, 0.2)), 0.3, 3.0)
    element_slot = jax.vmap(lambda own: jax.random.permutation(own, E_DEV))(jax.random.split(seeds[2], NS_TILES * NP_TILES)).reshape((NS_TILES, NP_TILES, E_DEV)).astype(jnp.int32)
    return {"right_side": right_side, "conductance": conductance, "element_slot": element_slot}


screening = 0.1
gll_points = [-1.0, -0.8717401485096066, -0.5917001814331423, -0.2092992179024789, 0.0, 0.2092992179024789, 0.5917001814331423, 0.8717401485096066, 1.0]


def legendre_seven(points_in):
    previous = np.ones(points_in.shape)
    current = np.array(points_in)
    for order in range(1, 7):
        following = ((2 * order + 1) * points_in * current - order * previous) / (order + 1)
        previous = current
        current = following
    return current


def gll_tables():
    degree = 7
    gll_nodes = np.array([gll_points[0], gll_points[1], gll_points[2], gll_points[3], gll_points[5], gll_points[6], gll_points[7], gll_points[8]])
    values = legendre_seven(gll_nodes)
    weights = 2.0 / (degree * (degree + 1) * values ** 2)
    points = degree + 1
    derivative = np.zeros((points, points))
    mass_matrix = np.zeros((points, points))
    mass_line = weights / 2.0
    for row_index in range(points):
        mass_matrix[row_index, row_index] = mass_line[row_index]
        for col_index in range(points):
            if row_index != col_index:
                derivative[row_index, col_index] = values[row_index] / (values[col_index] * (gll_nodes[row_index] - gll_nodes[col_index]))
    derivative[0, 0] = -degree * (degree + 1) / 4.0
    derivative[degree, degree] = degree * (degree + 1) / 4.0
    stiff_line = 2.0 * derivative.T @ (weights[:, None] * derivative)
    stiffness = np.kron(stiff_line, np.kron(mass_matrix, mass_matrix)) + np.kron(mass_matrix, np.kron(stiff_line, mass_matrix)) + np.kron(mass_matrix, np.kron(mass_matrix, stiff_line))
    mass_diag = np.kron(mass_line, np.kron(mass_line, mass_line))
    return stiffness, mass_diag


def fold_front(cube, wrap):
    element_count = cube.shape[0]
    tail_shape = cube.shape[2:]
    leading = cube[:, :7].reshape((element_count * 7,) + tail_shape)
    trailing = jnp.concatenate([cube[:, 7:], jnp.zeros((element_count, 6) + tail_shape, cube.dtype)], axis=1)
    trailing = trailing.reshape((element_count * 7,) + tail_shape)
    if wrap:
        return leading + jnp.roll(trailing, 7, axis=0)
    first_part = jnp.concatenate([leading, jnp.zeros((1,) + tail_shape, cube.dtype)], axis=0)
    second_part = jnp.concatenate([jnp.zeros((7,) + tail_shape, cube.dtype), trailing], axis=0)
    return first_part + second_part[: element_count * 7 + 1]


def unfold_front(grid, element_count, wrap):
    tail_shape = grid.shape[1:]
    leading = grid[: element_count * 7].reshape((element_count, 7) + tail_shape)
    if wrap:
        shifted = jnp.roll(grid, -7, axis=0)
    else:
        shifted = jnp.concatenate([grid[7:], jnp.zeros((6,) + tail_shape, grid.dtype)], axis=0)
    following = shifted.reshape((element_count, 7) + tail_shape)[:, :1]
    return jnp.concatenate([leading, following], axis=1)


def fold_at(cube, axis_pos, wrap):
    moved = jnp.moveaxis(cube, (axis_pos, axis_pos + 1), (0, 1))
    return jnp.moveaxis(fold_front(moved, wrap), 0, axis_pos)


def unfold_at(grid, axis_pos, element_count, wrap):
    moved = jnp.moveaxis(grid, axis_pos, 0)
    return jnp.moveaxis(unfold_front(moved, element_count, wrap), (0, 1), (axis_pos, axis_pos + 1))


def elements_to_grid(elements, count_x, count_y, count_z, wraps):
    cube = elements.reshape(count_x, count_y, count_z, 8, 8, 8).transpose(0, 3, 1, 4, 2, 5)
    cube = fold_at(cube, 4, wraps[2])
    cube = fold_at(cube, 2, wraps[1])
    return fold_at(cube, 0, wraps[0])


def grid_to_elements(grid, count_x, count_y, count_z, wraps):
    cube = unfold_at(grid, 0, count_x, wraps[0])
    cube = unfold_at(cube, 2, count_y, wraps[1])
    cube = unfold_at(cube, 4, count_z, wraps[2])
    return cube.transpose(0, 2, 4, 1, 3, 5).reshape(count_x * count_y * count_z, 512)


def reference(right_side, conductance, element_slot):
    stiff_np, mass_np = gll_tables()
    stiffness = jnp.asarray(stiff_np, jnp.float32)
    mass_diag = jnp.asarray(mass_np, jnp.float32)
    count_x = N_STREAM * TX
    count_y = N_SPAN * TY
    count_z = TZ
    wraps = (True, True, False)

    def to_global(values_in):
        picked = jax.vmap(jax.vmap(lambda block, order_in: block[order_in]))(values_in, element_slot)
        tail_shape = values_in.shape[3:]
        tiles = picked.reshape((N_STREAM, N_SPAN, TX, TY, TZ) + tail_shape)
        axes_order = (0, 2, 1, 3, 4) + tuple(range(5, 5 + len(tail_shape)))
        return tiles.transpose(axes_order).reshape((count_x * count_y * count_z,) + tail_shape)

    def to_slots(global_elements):
        tiles = global_elements.reshape(N_STREAM, TX, N_SPAN, TY, TZ, 512).transpose(0, 2, 1, 3, 4, 5)
        tiles = tiles.reshape(N_STREAM, N_SPAN, TX * TY * TZ, 512)
        return jax.vmap(jax.vmap(lambda block, order_in: jnp.zeros_like(block).at[order_in].set(block)))(tiles, element_slot)

    forcing = to_global(right_side)
    kappa = to_global(conductance)
    rhs = elements_to_grid(mass_diag[None, :] * forcing, count_x, count_y, count_z, wraps)
    diag_local = kappa[:, None] * jnp.diag(stiffness)[None, :] + screening * mass_diag[None, :]
    diag_grid = elements_to_grid(diag_local, count_x, count_y, count_z, wraps)

    def operate(grid_in):
        elements = grid_to_elements(grid_in, count_x, count_y, count_z, wraps)
        local = kappa[:, None] * jnp.dot(elements, stiffness, precision=lax.Precision.HIGHEST) + screening * mass_diag[None, :] * elements
        return elements_to_grid(local, count_x, count_y, count_z, wraps)

    solution = jnp.zeros_like(rhs)
    residual = rhs
    precond = residual / diag_grid
    direction = precond
    norm_now = jnp.sum(residual * precond)
    for iteration in range(ITERS):
        image = operate(direction)
        step_size = norm_now / jnp.sum(direction * image)
        solution = solution + step_size * direction
        residual = residual - step_size * image
        if iteration + 1 < ITERS:
            precond = residual / diag_grid
            norm_next = jnp.sum(residual * precond)
            direction = precond + (norm_next / norm_now) * direction
            norm_now = norm_next
    solution_elements = grid_to_elements(solution, count_x, count_y, count_z, wraps)
    residual_elements = grid_to_elements(residual, count_x, count_y, count_z, wraps)
    return to_slots(solution_elements), to_slots(residual_elements)
```

```python
import jax
import jax.numpy as jnp
import numpy as np
from jax import lax
from jax.sharding import PartitionSpec as P

TX = 2
TY = 2
TZ = 24
ITERS = 2


screening = 0.1
gll_points = [
    -1.0,
    -0.8717401485096066,
    -0.5917001814331423,
    -0.2092992179024789,
    0.0,
    0.2092992179024789,
    0.5917001814331423,
    0.8717401485096066,
    1.0,
]


def extended(cells, sides, width):
    for axis, dim in sides:
        count = lax.axis_size(axis)
        head = lax.slice_in_dim(cells, 0, width, axis=dim)
        tail = lax.slice_in_dim(cells, cells.shape[dim] - width, cells.shape[dim], axis=dim)
        cells = jnp.concatenate(
            [
                lax.ppermute(tail, axis, [(i, (i + 1) % count) for i in range(count)]),
                cells,
                lax.ppermute(head, axis, [((i + 1) % count, i) for i in range(count)]),
            ],
            axis=dim,
        )
    return cells


def legendre_seven(points_in):
    previous = np.ones(points_in.shape)
    current = np.array(points_in)
    for order in range(1, 7):
        following = ((2 * order + 1) * points_in * current - order * previous) / (order + 1)
        previous = current
        current = following
    return current


def gll_tables():
    degree = 7
    gll_nodes = np.array(
        [
            gll_points[0],
            gll_points[1],
            gll_points[2],
            gll_points[3],
            gll_points[5],
            gll_points[6],
            gll_points[7],
            gll_points[8],
        ]
    )
    values = legendre_seven(gll_nodes)
    weights = 2.0 / (degree * (degree + 1) * values**2)
    points = degree + 1
    derivative = np.zeros((points, points))
    mass_matrix = np.zeros((points, points))
    mass_line = weights / 2.0
    for row_index in range(points):
        mass_matrix[row_index, row_index] = mass_line[row_index]
        for col_index in range(points):
            if row_index != col_index:
                derivative[row_index, col_index] = values[row_index] / (
                    values[col_index] * (gll_nodes[row_index] - gll_nodes[col_index])
                )
    derivative[0, 0] = -degree * (degree + 1) / 4.0
    derivative[degree, degree] = degree * (degree + 1) / 4.0
    stiff_line = 2.0 * derivative.T @ (weights[:, None] * derivative)
    stiffness = (
        np.kron(stiff_line, np.kron(mass_matrix, mass_matrix))
        + np.kron(mass_matrix, np.kron(stiff_line, mass_matrix))
        + np.kron(mass_matrix, np.kron(mass_matrix, stiff_line))
    )
    mass_diag = np.kron(mass_line, np.kron(mass_line, mass_line))
    return (stiffness, mass_diag)


def node_weights(tiles_x, tiles_y, tiles_z):
    shared_ends = np.ones(8)
    shared_ends[0] = 2.0
    shared_ends[7] = 2.0
    vertical = np.ones((tiles_z, 8))
    vertical[1:, 0] = 2.0
    vertical[:-1, 7] = 2.0
    total = (
        shared_ends[None, :, None, None]
        * shared_ends[None, None, :, None]
        * vertical[:, None, None, :]
    )
    total = np.broadcast_to(total[None, None], (tiles_x, tiles_y, tiles_z, 8, 8, 8))
    return (1.0 / total).reshape(tiles_x * tiles_y * tiles_z, 512)


def fold_front(cube):
    element_count = cube.shape[0]
    tail_shape = cube.shape[2:]
    leading = cube[:, :7].reshape((element_count * 7,) + tail_shape)
    trailing = jnp.concatenate(
        [cube[:, 7:], jnp.zeros((element_count, 6) + tail_shape, cube.dtype)], axis=1
    )
    trailing = trailing.reshape((element_count * 7,) + tail_shape)
    first_part = jnp.concatenate([leading, jnp.zeros((1,) + tail_shape, cube.dtype)], axis=0)
    second_part = jnp.concatenate([jnp.zeros((7,) + tail_shape, cube.dtype), trailing], axis=0)
    return first_part + second_part[: element_count * 7 + 1]


def unfold_front(grid, element_count):
    tail_shape = grid.shape[1:]
    leading = grid[: element_count * 7].reshape((element_count, 7) + tail_shape)
    shifted = jnp.concatenate([grid[7:], jnp.zeros((6,) + tail_shape, grid.dtype)], axis=0)
    following = shifted.reshape((element_count, 7) + tail_shape)[:, :1]
    return jnp.concatenate([leading, following], axis=1)


def fold_at(cube, axis_pos):
    moved = jnp.moveaxis(cube, (axis_pos, axis_pos + 1), (0, 1))
    return jnp.moveaxis(fold_front(moved), 0, axis_pos)


def unfold_at(grid, axis_pos, element_count):
    moved = jnp.moveaxis(grid, axis_pos, 0)
    return jnp.moveaxis(unfold_front(moved, element_count), (0, 1), (axis_pos, axis_pos + 1))


def elements_to_grid(elements, count_x, count_y, count_z):
    cube = elements.reshape(count_x, count_y, count_z, 8, 8, 8).transpose(0, 3, 1, 4, 2, 5)
    cube = fold_at(cube, 4)
    cube = fold_at(cube, 2)
    return fold_at(cube, 0)


def grid_to_elements(grid, count_x, count_y, count_z):
    cube = unfold_at(grid, 0, count_x)
    cube = unfold_at(cube, 2, count_y)
    cube = unfold_at(cube, 4, count_z)
    return cube.transpose(0, 2, 4, 1, 3, 5).reshape(count_x * count_y * count_z, 512)


def assemble(stacked):
    grids = jax.vmap(lambda one_field: elements_to_grid(one_field, TX, TY, TZ))(stacked)
    padded = extended(grids, (("stream", 1), ("span", 2)), 1)
    partial_value = padded[:, 1:-1]
    partial_value = partial_value.at[:, 0].add(padded[:, 0]).at[:, -1].add(padded[:, -1])
    summed = partial_value[:, :, 1:-1]
    summed = (
        summed.at[:, :, 0].add(partial_value[:, :, 0]).at[:, :, -1].add(partial_value[:, :, -1])
    )
    return jax.vmap(lambda one_grid: grid_to_elements(one_grid, TX, TY, TZ))(summed)


def shards(right_side, conductance, element_slot):
    stiff_np, mass_np = gll_tables()
    stiffness = jnp.asarray(stiff_np, jnp.float32)
    mass_diag = jnp.asarray(mass_np, jnp.float32)
    weights = jnp.asarray(node_weights(TX, TY, TZ), jnp.float32)
    slot_index = element_slot[0, 0]
    forcing = right_side[0, 0][slot_index]
    kappa = conductance[0, 0][slot_index]

    def local_dot(first_vec, second_vec):
        return jnp.sum(first_vec * second_vec * weights)

    def apply_local(field):
        return (
            kappa[:, None] * jnp.dot(field, stiffness, precision=lax.Precision.HIGHEST)
            + screening * mass_diag[None, :] * field
        )

    diag_local = kappa[:, None] * jnp.diag(stiffness)[None, :] + screening * mass_diag[None, :]
    both = assemble(jnp.stack([mass_diag[None, :] * forcing, diag_local]))
    start_res = both[0]
    diag_field = both[1]
    start_z = start_res / diag_field
    first_image = assemble(apply_local(start_z)[None])[0]
    scaled_image = first_image / diag_field
    second_image = assemble(apply_local(scaled_image)[None])[0]
    sums = lax.psum(
        jnp.stack(
            [
                local_dot(start_res, start_z),
                local_dot(start_z, first_image),
                local_dot(start_res, scaled_image),
                local_dot(first_image, scaled_image),
                local_dot(start_z, second_image),
                local_dot(scaled_image, second_image),
            ]
        ),
        ("stream", "span"),
    )
    s_rz, s_zq, s_rw, s_qw, s_zp, s_wp = (sums[n] for n in range(6))
    alpha0 = s_rz / s_zq
    rz1 = s_rz - alpha0 * (s_rw + s_zq) + alpha0 * alpha0 * s_qw
    beta = rz1 / s_rz
    grow = 1.0 + beta
    dad1 = grow * grow * s_zq - alpha0 * grow * (s_zp + s_qw) + alpha0 * alpha0 * s_wp
    alpha1 = rz1 / dad1
    direction = grow * start_z - alpha0 * scaled_image
    image = grow * first_image - alpha0 * second_image
    solution = alpha0 * start_z + alpha1 * direction
    residual = (start_res - alpha0 * first_image) - alpha1 * image
    solution_out = jnp.zeros_like(solution).at[slot_index].set(solution)
    residual_out = jnp.zeros_like(residual).at[slot_index].set(residual)
    return (solution_out[None, None], residual_out[None, None])


def solution(mesh):
    placed = (P("stream", "span", None, None), P("stream", "span", None), P("stream", "span", None))
    return jax.shard_map(
        shards,
        mesh=mesh,
        in_specs=placed,
        out_specs=(P("stream", "span", None, None), P("stream", "span", None, None)),
        check_vma=False,
    )
```

```python
import jax
import jax.numpy as jnp
import numpy as np
from jax import lax
from jax.sharding import PartitionSpec as P

TX = 2
TY = 2
TZ = 24

screening = 0.1
gll_points = [
    -1.0,
    -0.8717401485096066,
    -0.5917001814331423,
    -0.2092992179024789,
    0.0,
    0.2092992179024789,
    0.5917001814331423,
    0.8717401485096066,
    1.0,
]


def legendre_seven(points_in):
    previous = np.ones(points_in.shape)
    current = np.array(points_in)
    for order in range(1, 7):
        following = ((2 * order + 1) * points_in * current - order * previous) / (order + 1)
        previous = current
        current = following
    return current


def gll_tables():
    degree = 7
    gll_nodes = np.array(
        [
            gll_points[0],
            gll_points[1],
            gll_points[2],
            gll_points[3],
            gll_points[5],
            gll_points[6],
            gll_points[7],
            gll_points[8],
        ]
    )
    values = legendre_seven(gll_nodes)
    weights = 2.0 / (degree * (degree + 1) * values**2)
    points = degree + 1
    derivative = np.zeros((points, points))
    mass_matrix = np.zeros((points, points))
    mass_line = weights / 2.0
    for row_index in range(points):
        mass_matrix[row_index, row_index] = mass_line[row_index]
        for col_index in range(points):
            if row_index != col_index:
                derivative[row_index, col_index] = values[row_index] / (
                    values[col_index] * (gll_nodes[row_index] - gll_nodes[col_index])
                )
    derivative[0, 0] = -degree * (degree + 1) / 4.0
    derivative[degree, degree] = degree * (degree + 1) / 4.0
    stiff_line = 2.0 * derivative.T @ (weights[:, None] * derivative)
    stiffness = (
        np.kron(stiff_line, np.kron(mass_matrix, mass_matrix))
        + np.kron(mass_matrix, np.kron(stiff_line, mass_matrix))
        + np.kron(mass_matrix, np.kron(mass_matrix, stiff_line))
    )
    mass_diag = np.kron(mass_line, np.kron(mass_line, mass_line))
    return (stiffness, mass_diag)


def node_weights(tiles_x, tiles_y, tiles_z):
    shared_ends = np.ones(8)
    shared_ends[0] = 2.0
    shared_ends[7] = 2.0
    vertical = np.ones((tiles_z, 8))
    vertical[1:, 0] = 2.0
    vertical[:-1, 7] = 2.0
    total = (
        shared_ends[None, :, None, None]
        * shared_ends[None, None, :, None]
        * vertical[:, None, None, :]
    )
    total = np.broadcast_to(total[None, None], (tiles_x, tiles_y, tiles_z, 8, 8, 8))
    return (1.0 / total).reshape(tiles_x * tiles_y * tiles_z, 512)


def lattice_masks():
    rows = np.arange(TX * TY * TZ)[:, None]
    lanes = np.arange(512)[None, :]
    layer = rows % TZ
    column = (rows // TZ) % TY
    node_x, node_y, node_z = lanes // 64, (lanes // 8) % 8, lanes % 8
    return {
        "z_up": (node_z == 7) & (layer < TZ - 1),
        "z_down": (node_z == 0) & (layer > 0),
        "x_up": (node_x == 7) & (rows < TY * TZ),
        "x_down": (node_x == 0) & (rows >= TY * TZ),
        "y_up": (node_y == 7) & (column == 0),
        "y_down": (node_y == 0) & (column == 1),
    }


def shifted(cells, rows, lanes):
    return jnp.roll(jnp.roll(cells, -rows, axis=1), -lanes, axis=2)


def exchange(face, axis, step):
    count = lax.axis_size(axis)
    return lax.ppermute(face, axis, [(i, (i + step) % count) for i in range(count)])


def assemble(stacked):
    masks = lattice_masks()
    zero = jnp.zeros((), stacked.dtype)
    half = TY * TZ
    cells = stacked
    cells = (
        cells
        + jnp.where(masks["z_up"], shifted(cells, 1, -7), zero)
        + jnp.where(masks["z_down"], shifted(cells, -1, 7), zero)
    )
    upper = cells[:, half:, 448:]
    lower = cells[:, :half, :64]
    from_prev = exchange(upper, "stream", 1)
    from_next = exchange(lower, "stream", -1)
    inner_x = jnp.where(masks["x_up"], shifted(cells, half, -448), zero) + jnp.where(
        masks["x_down"], shifted(cells, -half, 448), zero
    )
    cells = (
        cells
        + inner_x
        + jnp.pad(from_prev, ((0, 0), (0, half), (0, 448)))
        + jnp.pad(from_next, ((0, 0), (half, 0), (448, 0)))
    )
    count = stacked.shape[0]
    sheet = cells.reshape(count, TX, TY, TZ, 8, 8, 8)
    top = sheet[:, :, 1, :, :, 7, :]
    bottom = sheet[:, :, 0, :, :, 0, :]
    top_in = exchange(top, "span", 1)
    bottom_in = exchange(bottom, "span", -1)
    inner_y = jnp.where(masks["y_up"], shifted(cells, TZ, -56), zero) + jnp.where(
        masks["y_down"], shifted(cells, -TZ, 56), zero
    )
    pads_bottom = ((0, 0), (0, 0), (0, 1), (0, 0), (0, 0), (0, 7), (0, 0))
    pads_top = ((0, 0), (0, 0), (1, 0), (0, 0), (0, 0), (7, 0), (0, 0))
    place_bottom = jnp.pad(top_in[:, :, None, :, :, None, :], pads_bottom)
    place_top = jnp.pad(bottom_in[:, :, None, :, :, None, :], pads_top)
    outside = (place_bottom + place_top).reshape(cells.shape)
    return cells + inner_y + outside


def shards(right_side, conductance, element_slot):
    stiff_np, mass_np = gll_tables()
    stiffness = jnp.asarray(stiff_np, jnp.float32)
    mass_diag = jnp.asarray(mass_np, jnp.float32)
    weights = jnp.asarray(node_weights(TX, TY, TZ), jnp.float32)
    slot_index = element_slot[0, 0]
    picks = (slot_index[:, None] == jnp.arange(slot_index.shape[0])[None, :]).astype(jnp.float32)
    exact = lax.Precision.HIGHEST
    forcing = jnp.dot(picks, right_side[0, 0], precision=exact)
    kappa = jnp.dot(picks, conductance[0, 0][:, None], precision=exact)[:, 0]

    def local_dot(first_vec, second_vec):
        return jnp.sum(first_vec * second_vec * weights)

    def apply_local(field):
        return (
            kappa[:, None] * jnp.dot(field, stiffness, precision=lax.Precision.HIGHEST)
            + screening * mass_diag[None, :] * field
        )

    diag_local = kappa[:, None] * jnp.diag(stiffness)[None, :] + screening * mass_diag[None, :]
    both = assemble(jnp.stack([mass_diag[None, :] * forcing, diag_local]))
    start_res = both[0]
    diag_field = both[1]
    start_z = start_res / diag_field
    first_image = assemble(apply_local(start_z)[None])[0]
    scaled_image = first_image / diag_field
    second_image = assemble(apply_local(scaled_image)[None])[0]
    sums = lax.psum(
        jnp.stack(
            [
                local_dot(start_res, start_z),
                local_dot(start_z, first_image),
                local_dot(start_res, scaled_image),
                local_dot(first_image, scaled_image),
                local_dot(start_z, second_image),
                local_dot(scaled_image, second_image),
            ]
        ),
        ("stream", "span"),
    )
    s_rz, s_zq, s_rw, s_qw, s_zp, s_wp = (sums[n] for n in range(6))
    alpha0 = s_rz / s_zq
    rz1 = s_rz - alpha0 * (s_rw + s_zq) + alpha0 * alpha0 * s_qw
    beta = rz1 / s_rz
    grow = 1.0 + beta
    dad1 = grow * grow * s_zq - alpha0 * grow * (s_zp + s_qw) + alpha0 * alpha0 * s_wp
    alpha1 = rz1 / dad1
    direction = grow * start_z - alpha0 * scaled_image
    image = grow * first_image - alpha0 * second_image
    solution = alpha0 * start_z + alpha1 * direction
    residual = (start_res - alpha0 * first_image) - alpha1 * image
    both_out = jnp.dot(picks.T, jnp.concatenate([solution, residual], axis=1), precision=exact)
    solution_out = both_out[:, : solution.shape[1]]
    residual_out = both_out[:, solution.shape[1] :]
    return (solution_out[None, None], residual_out[None, None])


def solution(mesh):
    placed = (P("stream", "span", None, None), P("stream", "span", None), P("stream", "span", None))
    return jax.shard_map(
        shards,
        mesh=mesh,
        in_specs=placed,
        out_specs=(P("stream", "span", None, None), P("stream", "span", None, None)),
        check_vma=False,
    )
```

```python
import jax
import jax.numpy as jnp
import numpy as np
from jax import lax
from jax.sharding import PartitionSpec as P

TX = 2
TY = 2
TZ = 24

screening = 0.1
gll_points = [
    -1.0,
    -0.8717401485096066,
    -0.5917001814331423,
    -0.2092992179024789,
    0.0,
    0.2092992179024789,
    0.5917001814331423,
    0.8717401485096066,
    1.0,
]


def legendre_seven(points_in):
    previous = np.ones(points_in.shape)
    current = np.array(points_in)
    for order in range(1, 7):
        following = ((2 * order + 1) * points_in * current - order * previous) / (order + 1)
        previous = current
        current = following
    return current


def gll_tables():
    degree = 7
    gll_nodes = np.array(
        [
            gll_points[0],
            gll_points[1],
            gll_points[2],
            gll_points[3],
            gll_points[5],
            gll_points[6],
            gll_points[7],
            gll_points[8],
        ]
    )
    values = legendre_seven(gll_nodes)
    weights = 2.0 / (degree * (degree + 1) * values**2)
    points = degree + 1
    derivative = np.zeros((points, points))
    mass_matrix = np.zeros((points, points))
    mass_line = weights / 2.0
    for row_index in range(points):
        mass_matrix[row_index, row_index] = mass_line[row_index]
        for col_index in range(points):
            if row_index != col_index:
                derivative[row_index, col_index] = values[row_index] / (
                    values[col_index] * (gll_nodes[row_index] - gll_nodes[col_index])
                )
    derivative[0, 0] = -degree * (degree + 1) / 4.0
    derivative[degree, degree] = degree * (degree + 1) / 4.0
    stiff_line = 2.0 * derivative.T @ (weights[:, None] * derivative)
    stiffness = (
        np.kron(stiff_line, np.kron(mass_matrix, mass_matrix))
        + np.kron(mass_matrix, np.kron(stiff_line, mass_matrix))
        + np.kron(mass_matrix, np.kron(mass_matrix, stiff_line))
    )
    mass_diag = np.kron(mass_line, np.kron(mass_line, mass_line))
    return (stiffness, mass_diag)


def node_weights(tiles_x, tiles_y, tiles_z):
    shared_ends = np.ones(8)
    shared_ends[0] = 2.0
    shared_ends[7] = 2.0
    vertical = np.ones((tiles_z, 8))
    vertical[1:, 0] = 2.0
    vertical[:-1, 7] = 2.0
    total = (
        shared_ends[None, :, None, None]
        * shared_ends[None, None, :, None]
        * vertical[:, None, None, :]
    )
    total = np.broadcast_to(total[None, None], (tiles_x, tiles_y, tiles_z, 8, 8, 8))
    return (1.0 / total).reshape(tiles_x * tiles_y * tiles_z, 512)


def lattice_masks():
    rows = np.arange(TX * TY * TZ)[:, None]
    lanes = np.arange(512)[None, :]
    layer = rows % TZ
    column = (rows // TZ) % TY
    node_x, node_y, node_z = lanes // 64, (lanes // 8) % 8, lanes % 8
    return {
        "z_up": (node_z == 7) & (layer < TZ - 1),
        "z_down": (node_z == 0) & (layer > 0),
        "x_up": (node_x == 7) & (rows < TY * TZ),
        "x_down": (node_x == 0) & (rows >= TY * TZ),
        "y_up": (node_y == 7) & (column == 0),
        "y_down": (node_y == 0) & (column == 1),
    }


def shifted(cells, rows, lanes):
    return jnp.roll(jnp.roll(cells, -rows, axis=1), -lanes, axis=2)


def exchange(face, axis, step):
    count = lax.axis_size(axis)
    return lax.ppermute(face, axis, [(i, (i + step) % count) for i in range(count)])


def assemble(stacked):
    masks = lattice_masks()
    zero = jnp.zeros((), stacked.dtype)
    half = TY * TZ
    cells = stacked
    cells = (
        cells
        + jnp.where(masks["z_up"], shifted(cells, 1, -7), zero)
        + jnp.where(masks["z_down"], shifted(cells, -1, 7), zero)
    )
    upper = cells[:, half:, 448:]
    lower = cells[:, :half, :64]
    from_prev = exchange(upper, "stream", 1)
    from_next = exchange(lower, "stream", -1)
    inner_x = jnp.where(masks["x_up"], shifted(cells, half, -448), zero) + jnp.where(
        masks["x_down"], shifted(cells, -half, 448), zero
    )
    cells = (
        cells
        + inner_x
        + jnp.pad(from_prev, ((0, 0), (0, half), (0, 448)))
        + jnp.pad(from_next, ((0, 0), (half, 0), (448, 0)))
    )
    count = stacked.shape[0]
    sheet = cells.reshape(count, TX, TY, TZ, 8, 8, 8)
    top = sheet[:, :, 1, :, :, 7, :]
    bottom = sheet[:, :, 0, :, :, 0, :]
    top_in = exchange(top, "span", 1)
    bottom_in = exchange(bottom, "span", -1)
    inner_y = jnp.where(masks["y_up"], shifted(cells, TZ, -56), zero) + jnp.where(
        masks["y_down"], shifted(cells, -TZ, 56), zero
    )
    pads_bottom = ((0, 0), (0, 0), (0, 1), (0, 0), (0, 0), (0, 7), (0, 0))
    pads_top = ((0, 0), (0, 0), (1, 0), (0, 0), (0, 0), (7, 0), (0, 0))
    place_bottom = jnp.pad(top_in[:, :, None, :, :, None, :], pads_bottom)
    place_top = jnp.pad(bottom_in[:, :, None, :, :, None, :], pads_top)
    outside = (place_bottom + place_top).reshape(cells.shape)
    return cells + inner_y + outside


def moved(value, axis, stride, count, shift):
    size = lax.axis_size(axis)
    pairs = []
    for index in range(size):
        spot = (index // stride) % count
        pairs.append((index, index + ((spot + shift) % count - spot) * stride))
    return lax.ppermute(value, axis, pairs)


def group_sum(value, axis, stride, count):
    total, width, windows = value, 1, {1: value}
    while width * 2 <= count:
        total = total + moved(total, axis, stride, count, width)
        width *= 2
        windows[width] = total
    rest, shift = count - width, width
    for size in sorted(windows, reverse=True):
        if rest >= size:
            total = total + moved(windows[size], axis, stride, count, shift)
            shift += size
            rest -= size
    return total


def global_sum(value):
    streams = lax.axis_size("stream")
    if streams % 16 == 0:
        groups = ((1, 2), (2, 8), (16, streams // 16))
    else:
        groups = ((1, streams),)
    for stride, count in groups:
        if count > 1:
            value = group_sum(value, "stream", stride, count)
    return group_sum(value, "span", 1, lax.axis_size("span"))


def shards(right_side, conductance, element_slot):
    stiff_np, mass_np = gll_tables()
    stiffness = jnp.asarray(stiff_np, jnp.float32)
    mass_diag = jnp.asarray(mass_np, jnp.float32)
    weights = jnp.asarray(node_weights(TX, TY, TZ), jnp.float32)
    slot_index = element_slot[0, 0]
    picks = (slot_index[:, None] == jnp.arange(slot_index.shape[0])[None, :]).astype(jnp.float32)
    exact = lax.Precision.HIGHEST
    forcing = jnp.dot(picks, right_side[0, 0], precision=exact)
    kappa = jnp.dot(picks, conductance[0, 0][:, None], precision=exact)[:, 0]

    def local_dot(first_vec, second_vec):
        return jnp.sum(first_vec * second_vec * weights)

    def apply_local(field):
        return (
            kappa[:, None] * jnp.dot(field, stiffness, precision=lax.Precision.HIGHEST)
            + screening * mass_diag[None, :] * field
        )

    stiff_diag = jnp.asarray(np.diag(stiff_np), jnp.float32)
    diag_local = kappa[:, None] * stiff_diag[None, :] + screening * mass_diag[None, :]
    both = assemble(jnp.stack([mass_diag[None, :] * forcing, diag_local]))
    start_res = both[0]
    diag_field = both[1]
    start_z = start_res / diag_field
    first_local = apply_local(start_z)
    first_image = assemble(first_local[None])[0]
    scaled_image = first_image / diag_field
    second_local = apply_local(scaled_image)
    sums = global_sum(
        jnp.stack(
            [
                local_dot(start_res, start_z),
                jnp.sum(start_z * first_local),
                local_dot(start_res, scaled_image),
                local_dot(first_image, scaled_image),
                jnp.sum(start_z * second_local),
                jnp.sum(scaled_image * second_local),
            ]
        )
    )
    second_image = assemble(second_local[None])[0]
    s_rz, s_zq, s_rw, s_qw, s_zp, s_wp = (sums[n] for n in range(6))
    alpha0 = s_rz / s_zq
    rz1 = s_rz - alpha0 * (s_rw + s_zq) + alpha0 * alpha0 * s_qw
    beta = rz1 / s_rz
    grow = 1.0 + beta
    dad1 = grow * grow * s_zq - alpha0 * grow * (s_zp + s_qw) + alpha0 * alpha0 * s_wp
    alpha1 = rz1 / dad1
    direction = grow * start_z - alpha0 * scaled_image
    image = grow * first_image - alpha0 * second_image
    solution = alpha0 * start_z + alpha1 * direction
    residual = (start_res - alpha0 * first_image) - alpha1 * image
    both_out = jnp.dot(picks.T, jnp.concatenate([solution, residual], axis=1), precision=exact)
    solution_out = both_out[:, : solution.shape[1]]
    residual_out = both_out[:, solution.shape[1] :]
    return (solution_out[None, None], residual_out[None, None])


def solution(mesh):
    placed = (P("stream", "span", None, None), P("stream", "span", None), P("stream", "span", None))
    return jax.shard_map(
        shards,
        mesh=mesh,
        in_specs=placed,
        out_specs=(P("stream", "span", None, None), P("stream", "span", None, None)),
        check_vma=False,
    )
```

```python
import jax
import jax.numpy as jnp
import numpy as np
from jax import lax
from jax.sharding import PartitionSpec as P

TX = 2
TY = 2
TZ = 24

screening = 0.1
gll_points = [
    -1.0,
    -0.8717401485096066,
    -0.5917001814331423,
    -0.2092992179024789,
    0.0,
    0.2092992179024789,
    0.5917001814331423,
    0.8717401485096066,
    1.0,
]


def legendre_seven(points_in):
    previous = np.ones(points_in.shape)
    current = np.array(points_in)
    for order in range(1, 7):
        following = ((2 * order + 1) * points_in * current - order * previous) / (order + 1)
        previous = current
        current = following
    return current


def gll_tables():
    degree = 7
    gll_nodes = np.array(
        [
            gll_points[0],
            gll_points[1],
            gll_points[2],
            gll_points[3],
            gll_points[5],
            gll_points[6],
            gll_points[7],
            gll_points[8],
        ]
    )
    values = legendre_seven(gll_nodes)
    weights = 2.0 / (degree * (degree + 1) * values**2)
    points = degree + 1
    derivative = np.zeros((points, points))
    mass_matrix = np.zeros((points, points))
    mass_line = weights / 2.0
    for row_index in range(points):
        mass_matrix[row_index, row_index] = mass_line[row_index]
        for col_index in range(points):
            if row_index != col_index:
                derivative[row_index, col_index] = values[row_index] / (
                    values[col_index] * (gll_nodes[row_index] - gll_nodes[col_index])
                )
    derivative[0, 0] = -degree * (degree + 1) / 4.0
    derivative[degree, degree] = degree * (degree + 1) / 4.0
    stiff_line = 2.0 * derivative.T @ (weights[:, None] * derivative)
    stiffness = (
        np.kron(stiff_line, np.kron(mass_matrix, mass_matrix))
        + np.kron(mass_matrix, np.kron(stiff_line, mass_matrix))
        + np.kron(mass_matrix, np.kron(mass_matrix, stiff_line))
    )
    mass_diag = np.kron(mass_line, np.kron(mass_line, mass_line))
    return (stiffness, mass_diag)


def node_weights(tiles_x, tiles_y, tiles_z):
    shared_ends = np.ones(8)
    shared_ends[0] = 2.0
    shared_ends[7] = 2.0
    vertical = np.ones((tiles_z, 8))
    vertical[1:, 0] = 2.0
    vertical[:-1, 7] = 2.0
    total = (
        shared_ends[None, :, None, None]
        * shared_ends[None, None, :, None]
        * vertical[:, None, None, :]
    )
    total = np.broadcast_to(total[None, None], (tiles_x, tiles_y, tiles_z, 8, 8, 8))
    return (1.0 / total).reshape(tiles_x * tiles_y * tiles_z, 512)


def lattice_masks():
    rows = np.arange(TX * TY * TZ)[:, None]
    lanes = np.arange(512)[None, :]
    layer = rows % TZ
    column = (rows // TZ) % TY
    node_x, node_y, node_z = lanes // 64, (lanes // 8) % 8, lanes % 8
    return {
        "z_up": (node_z == 7) & (layer < TZ - 1),
        "z_down": (node_z == 0) & (layer > 0),
        "x_up": (node_x == 7) & (rows < TY * TZ),
        "x_down": (node_x == 0) & (rows >= TY * TZ),
        "y_up": (node_y == 7) & (column == 0),
        "y_down": (node_y == 0) & (column == 1),
    }


def shifted(cells, rows, lanes):
    return jnp.roll(jnp.roll(cells, -rows, axis=1), -lanes, axis=2)


def exchange(face, axis, step):
    count = lax.axis_size(axis)
    return lax.ppermute(face, axis, [(i, (i + step) % count) for i in range(count)])


def send_x(stacked):
    masks = lattice_masks()
    zero = jnp.zeros((), stacked.dtype)
    half = TY * TZ
    cells = stacked
    cells = (
        cells
        + jnp.where(masks["z_up"], shifted(cells, 1, -7), zero)
        + jnp.where(masks["z_down"], shifted(cells, -1, 7), zero)
    )
    from_prev = exchange(cells[:, half:, 448:], "stream", 1)
    from_next = exchange(cells[:, :half, :64], "stream", -1)
    return cells, (from_prev, from_next)


def send_y(cells, faces):
    masks = lattice_masks()
    zero = jnp.zeros((), cells.dtype)
    half = TY * TZ
    from_prev, from_next = faces
    inner_x = jnp.where(masks["x_up"], shifted(cells, half, -448), zero) + jnp.where(
        masks["x_down"], shifted(cells, -half, 448), zero
    )
    cells = (
        cells
        + inner_x
        + jnp.pad(from_prev, ((0, 0), (0, half), (0, 448)))
        + jnp.pad(from_next, ((0, 0), (half, 0), (448, 0)))
    )
    sheet = cells.reshape(cells.shape[0], TX, TY, TZ, 8, 8, 8)
    top_in = exchange(sheet[:, :, 1, :, :, 7, :], "span", 1)
    bottom_in = exchange(sheet[:, :, 0, :, :, 0, :], "span", -1)
    return cells, (top_in, bottom_in)


def finish_y(cells, faces):
    masks = lattice_masks()
    zero = jnp.zeros((), cells.dtype)
    top_in, bottom_in = faces
    inner_y = jnp.where(masks["y_up"], shifted(cells, TZ, -56), zero) + jnp.where(
        masks["y_down"], shifted(cells, -TZ, 56), zero
    )
    pads_bottom = ((0, 0), (0, 0), (0, 1), (0, 0), (0, 0), (0, 7), (0, 0))
    pads_top = ((0, 0), (0, 0), (1, 0), (0, 0), (0, 0), (7, 0), (0, 0))
    place_bottom = jnp.pad(top_in[:, :, None, :, :, None, :], pads_bottom)
    place_top = jnp.pad(bottom_in[:, :, None, :, :, None, :], pads_top)
    outside = (place_bottom + place_top).reshape(cells.shape)
    return cells + inner_y + outside


def assemble(stacked):
    return finish_y(*send_y(*send_x(stacked)))


def moved(value, axis, stride, count, shift):
    size = lax.axis_size(axis)
    pairs = []
    for index in range(size):
        spot = (index // stride) % count
        pairs.append((index, index + ((spot + shift) % count - spot) * stride))
    return lax.ppermute(value, axis, pairs)


def group_sum(value, axis, stride, count, after_round):
    unit, units, total = 1, count, value
    if count % 3 == 0:
        total = value + moved(value, axis, stride, count, 1) + moved(value, axis, stride, count, -1)
        total = after_round(total)
        unit, units = 3, count // 3
    width, windows = 1, {1: total}
    while width * 2 <= units:
        total = total + moved(total, axis, stride, count, width * unit)
        total = after_round(total)
        width *= 2
        windows[width] = total
    rest, shift = units - width, width
    for size in sorted(windows, reverse=True):
        if rest >= size:
            total = total + moved(windows[size], axis, stride, count, shift * unit)
            total = after_round(total)
            shift += size
            rest -= size
    return total


def global_sum(value, hooks):
    streams = lax.axis_size("stream")
    if streams % 16 == 0:
        groups = ((1, 2), (2, 8), (16, streams // 16))
    else:
        groups = ((1, streams),)
    done = [0]

    def after_round(total):
        done[0] += 1
        hook = hooks.get(done[0])
        return total if hook is None else hook(total)

    for stride, count in groups:
        if count > 1:
            value = group_sum(value, "stream", stride, count, after_round)
    return group_sum(value, "span", 1, lax.axis_size("span"), after_round)


def shards(right_side, conductance, element_slot):
    stiff_np, mass_np = gll_tables()
    stiffness = jnp.asarray(stiff_np, jnp.float32)
    mass_diag = jnp.asarray(mass_np, jnp.float32)
    weights = jnp.asarray(node_weights(TX, TY, TZ), jnp.float32)
    slot_index = element_slot[0, 0]
    picks = (slot_index[:, None] == jnp.arange(slot_index.shape[0])[None, :]).astype(jnp.float32)
    exact = lax.Precision.HIGHEST
    forcing = jnp.dot(picks, right_side[0, 0], precision=exact)
    kappa = jnp.dot(picks, conductance[0, 0][:, None], precision=exact)[:, 0]

    def local_dot(first_vec, second_vec):
        return jnp.sum(first_vec * second_vec * weights)

    def apply_local(field):
        return (
            kappa[:, None] * jnp.dot(field, stiffness, precision=lax.Precision.HIGHEST)
            + screening * mass_diag[None, :] * field
        )

    stiff_diag = jnp.asarray(np.diag(stiff_np), jnp.float32)
    diag_local = kappa[:, None] * stiff_diag[None, :] + screening * mass_diag[None, :]
    both = assemble(jnp.stack([mass_diag[None, :] * forcing, diag_local]))
    start_res = both[0]
    diag_field = both[1]
    start_z = start_res / diag_field
    first_local = apply_local(start_z)
    first_image = assemble(first_local[None])[0]
    scaled_image = first_image / diag_field
    second_local = apply_local(scaled_image)
    products = jnp.stack(
        [
            start_res * start_z * weights,
            start_z * first_local,
            start_res * scaled_image * weights,
            first_image * scaled_image * weights,
            start_z * second_local,
            scaled_image * second_local,
        ]
    )
    stage = {}
    stage["x"] = send_x(second_local[None])

    def after_x(total):
        total, faces = lax.optimization_barrier((total, stage["x"][1]))
        stage["y"] = send_y(stage["x"][0], faces)
        return total

    def after_y(total):
        total, faces = lax.optimization_barrier((total, stage["y"][1]))
        stage["y"] = (stage["y"][0], faces)
        return total

    sums = global_sum(jnp.sum(products, axis=(1, 2)), {2: after_x, 5: after_y})
    if "y" not in stage:
        stage["y"] = send_y(*stage["x"])
    second_image = finish_y(*stage["y"])[0]
    s_rz, s_zq, s_rw, s_qw, s_zp, s_wp = (sums[n] for n in range(6))
    alpha0 = s_rz / s_zq
    rz1 = s_rz - alpha0 * (s_rw + s_zq) + alpha0 * alpha0 * s_qw
    beta = rz1 / s_rz
    grow = 1.0 + beta
    dad1 = grow * grow * s_zq - alpha0 * grow * (s_zp + s_qw) + alpha0 * alpha0 * s_wp
    alpha1 = rz1 / dad1
    direction = grow * start_z - alpha0 * scaled_image
    image = grow * first_image - alpha0 * second_image
    solution = alpha0 * start_z + alpha1 * direction
    residual = (start_res - alpha0 * first_image) - alpha1 * image
    both_out = jnp.dot(picks.T, jnp.concatenate([solution, residual], axis=1), precision=exact)
    solution_out = both_out[:, : solution.shape[1]]
    residual_out = both_out[:, solution.shape[1] :]
    return (solution_out[None, None], residual_out[None, None])


def solution(mesh):
    placed = (P("stream", "span", None, None), P("stream", "span", None), P("stream", "span", None))
    return jax.shard_map(
        shards,
        mesh=mesh,
        in_specs=placed,
        out_specs=(P("stream", "span", None, None), P("stream", "span", None, None)),
        check_vma=False,
    )
```

```python
import jax
import jax.numpy as jnp
import numpy as np
from jax import lax
from jax.sharding import PartitionSpec as P

TX = 2
TY = 2
TZ = 24

screening = 0.1
gll_points = [
    -1.0,
    -0.8717401485096066,
    -0.5917001814331423,
    -0.2092992179024789,
    0.0,
    0.2092992179024789,
    0.5917001814331423,
    0.8717401485096066,
    1.0,
]


def legendre_seven(points_in):
    previous = np.ones(points_in.shape)
    current = np.array(points_in)
    for order in range(1, 7):
        following = ((2 * order + 1) * points_in * current - order * previous) / (order + 1)
        previous = current
        current = following
    return current


def gll_tables():
    degree = 7
    gll_nodes = np.array(
        [
            gll_points[0],
            gll_points[1],
            gll_points[2],
            gll_points[3],
            gll_points[5],
            gll_points[6],
            gll_points[7],
            gll_points[8],
        ]
    )
    values = legendre_seven(gll_nodes)
    weights = 2.0 / (degree * (degree + 1) * values**2)
    points = degree + 1
    derivative = np.zeros((points, points))
    mass_matrix = np.zeros((points, points))
    mass_line = weights / 2.0
    for row_index in range(points):
        mass_matrix[row_index, row_index] = mass_line[row_index]
        for col_index in range(points):
            if row_index != col_index:
                derivative[row_index, col_index] = values[row_index] / (
                    values[col_index] * (gll_nodes[row_index] - gll_nodes[col_index])
                )
    derivative[0, 0] = -degree * (degree + 1) / 4.0
    derivative[degree, degree] = degree * (degree + 1) / 4.0
    stiff_line = 2.0 * derivative.T @ (weights[:, None] * derivative)
    stiffness = (
        np.kron(stiff_line, np.kron(mass_matrix, mass_matrix))
        + np.kron(mass_matrix, np.kron(stiff_line, mass_matrix))
        + np.kron(mass_matrix, np.kron(mass_matrix, stiff_line))
    )
    mass_diag = np.kron(mass_line, np.kron(mass_line, mass_line))
    return (stiffness, mass_diag)


def node_weights(tiles_x, tiles_y, tiles_z):
    shared_ends = np.ones(8)
    shared_ends[0] = 2.0
    shared_ends[7] = 2.0
    vertical = np.ones((tiles_z, 8))
    vertical[1:, 0] = 2.0
    vertical[:-1, 7] = 2.0
    total = (
        shared_ends[None, :, None, None]
        * shared_ends[None, None, :, None]
        * vertical[:, None, None, :]
    )
    total = np.broadcast_to(total[None, None], (tiles_x, tiles_y, tiles_z, 8, 8, 8))
    return (1.0 / total).reshape(tiles_x * tiles_y * tiles_z, 512)


def lattice_masks():
    rows = np.arange(TX * TY * TZ)[:, None]
    lanes = np.arange(512)[None, :]
    layer = rows % TZ
    column = (rows // TZ) % TY
    node_x, node_y, node_z = lanes // 64, (lanes // 8) % 8, lanes % 8
    return {
        "z_up": (node_z == 7) & (layer < TZ - 1),
        "z_down": (node_z == 0) & (layer > 0),
        "x_up": (node_x == 7) & (rows < TY * TZ),
        "x_down": (node_x == 0) & (rows >= TY * TZ),
        "y_up": (node_y == 7) & (column == 0),
        "y_down": (node_y == 0) & (column == 1),
    }


def shifted(cells, rows, lanes):
    return jnp.roll(jnp.roll(cells, -rows, axis=1), -lanes, axis=2)


def exchange(face, axis, step):
    count = lax.axis_size(axis)
    return lax.ppermute(face, axis, [(i, (i + step) % count) for i in range(count)])


def assemble(stacked):
    masks = lattice_masks()
    zero = jnp.zeros((), stacked.dtype)
    half = TY * TZ
    cells = stacked
    cells = (
        cells
        + jnp.where(masks["z_up"], shifted(cells, 1, -7), zero)
        + jnp.where(masks["z_down"], shifted(cells, -1, 7), zero)
    )
    upper = cells[:, half:, 448:]
    lower = cells[:, :half, :64]
    from_prev = exchange(upper, "stream", 1)
    from_next = exchange(lower, "stream", -1)
    inner_x = jnp.where(masks["x_up"], shifted(cells, half, -448), zero) + jnp.where(
        masks["x_down"], shifted(cells, -half, 448), zero
    )
    cells = (
        cells
        + inner_x
        + jnp.pad(from_prev, ((0, 0), (0, half), (0, 448)))
        + jnp.pad(from_next, ((0, 0), (half, 0), (448, 0)))
    )
    count = stacked.shape[0]
    sheet = cells.reshape(count, TX, TY, TZ, 8, 8, 8)
    top = sheet[:, :, 1, :, :, 7, :]
    bottom = sheet[:, :, 0, :, :, 0, :]
    top_in = exchange(top, "span", 1)
    bottom_in = exchange(bottom, "span", -1)
    inner_y = jnp.where(masks["y_up"], shifted(cells, TZ, -56), zero) + jnp.where(
        masks["y_down"], shifted(cells, -TZ, 56), zero
    )
    pads_bottom = ((0, 0), (0, 0), (0, 1), (0, 0), (0, 0), (0, 7), (0, 0))
    pads_top = ((0, 0), (0, 0), (1, 0), (0, 0), (0, 0), (7, 0), (0, 0))
    place_bottom = jnp.pad(top_in[:, :, None, :, :, None, :], pads_bottom)
    place_top = jnp.pad(bottom_in[:, :, None, :, :, None, :], pads_top)
    outside = (place_bottom + place_top).reshape(cells.shape)
    return cells + inner_y + outside


def moved(value, axis, stride, count, shift):
    size = lax.axis_size(axis)
    pairs = []
    for index in range(size):
        spot = (index // stride) % count
        pairs.append((index, index + ((spot + shift) % count - spot) * stride))
    return lax.ppermute(value, axis, pairs)


def group_sum(value, axis, stride, count):
    total, width, windows = value, 1, {1: value}
    while width * 2 <= count:
        total = total + moved(total, axis, stride, count, width)
        width *= 2
        windows[width] = total
    rest, shift = count - width, width
    for size in sorted(windows, reverse=True):
        if rest >= size:
            total = total + moved(windows[size], axis, stride, count, shift)
            shift += size
            rest -= size
    return total


def global_sum(value):
    streams = lax.axis_size("stream")
    if streams % 16 == 0:
        groups = ((1, 2), (2, 8), (16, streams // 16))
    else:
        groups = ((1, streams),)
    for stride, count in groups:
        if count > 1:
            value = group_sum(value, "stream", stride, count)
    return group_sum(value, "span", 1, lax.axis_size("span"))


def shards(right_side, conductance, element_slot):
    stiff_np, mass_np = gll_tables()
    stiffness = jnp.asarray(stiff_np, jnp.float32)
    mass_diag = jnp.asarray(mass_np, jnp.float32)
    weights = jnp.asarray(node_weights(TX, TY, TZ), jnp.float32)
    slot_index = element_slot[0, 0]
    picks = (slot_index[:, None] == jnp.arange(slot_index.shape[0])[None, :]).astype(jnp.float32)
    exact = lax.Precision.HIGHEST
    forcing = jnp.dot(picks, right_side[0, 0], precision=exact)
    kappa = jnp.dot(picks, conductance[0, 0][:, None], precision=exact)[:, 0]

    def local_dot(first_vec, second_vec):
        return jnp.sum(first_vec * second_vec * weights)

    def apply_local(field):
        return (
            kappa[:, None] * jnp.dot(field, stiffness, precision=lax.Precision.HIGHEST)
            + screening * mass_diag[None, :] * field
        )

    stiff_diag = jnp.asarray(np.diag(stiff_np), jnp.float32)
    diag_local = kappa[:, None] * stiff_diag[None, :] + screening * mass_diag[None, :]
    both = assemble(jnp.stack([mass_diag[None, :] * forcing, diag_local]))
    start_res = both[0]
    diag_field = both[1]
    start_z = start_res / diag_field
    first_local = apply_local(start_z)
    first_image = assemble(first_local[None])[0]
    scaled_image = first_image / diag_field
    second_local = apply_local(scaled_image)
    lane_sums = jnp.stack(
        [
            jnp.sum(start_res * start_z * weights, axis=0),
            jnp.sum(start_z * first_local, axis=0),
            jnp.sum(start_res * scaled_image * weights, axis=0),
            jnp.sum(first_image * scaled_image * weights, axis=0),
            jnp.sum(start_z * second_local, axis=0),
            jnp.sum(scaled_image * second_local, axis=0),
        ]
    )
    span = lane_sums.shape[1] // 2
    while span >= 1:
        lane_sums = lane_sums + jnp.roll(lane_sums, span, axis=1)
        span //= 2
    sums = global_sum(lane_sums)
    second_image = assemble(second_local[None])[0]
    s_rz, s_zq, s_rw, s_qw, s_zp, s_wp = (sums[n] for n in range(6))
    alpha0 = s_rz / s_zq
    rz1 = s_rz - alpha0 * (s_rw + s_zq) + alpha0 * alpha0 * s_qw
    beta = rz1 / s_rz
    grow = 1.0 + beta
    dad1 = grow * grow * s_zq - alpha0 * grow * (s_zp + s_qw) + alpha0 * alpha0 * s_wp
    alpha1 = rz1 / dad1
    alpha0, grow, alpha1 = alpha0[None, :], grow[None, :], alpha1[None, :]
    direction = grow * start_z - alpha0 * scaled_image
    image = grow * first_image - alpha0 * second_image
    solution = alpha0 * start_z + alpha1 * direction
    residual = (start_res - alpha0 * first_image) - alpha1 * image
    both_out = jnp.dot(picks.T, jnp.concatenate([solution, residual], axis=1), precision=exact)
    solution_out = both_out[:, : solution.shape[1]]
    residual_out = both_out[:, solution.shape[1] :]
    return (solution_out[None, None], residual_out[None, None])


def solution(mesh):
    placed = (P("stream", "span", None, None), P("stream", "span", None), P("stream", "span", None))
    return jax.shard_map(
        shards,
        mesh=mesh,
        in_specs=placed,
        out_specs=(P("stream", "span", None, None), P("stream", "span", None, None)),
        check_vma=False,
    )
```

```python
import jax
import jax.numpy as jnp
import numpy as np
from jax import lax
from jax.sharding import PartitionSpec as P

TX = 2
TY = 2
TZ = 24

screening = 0.1
gll_points = [
    -1.0,
    -0.8717401485096066,
    -0.5917001814331423,
    -0.2092992179024789,
    0.0,
    0.2092992179024789,
    0.5917001814331423,
    0.8717401485096066,
    1.0,
]


def legendre_seven(points_in):
    previous = np.ones(points_in.shape)
    current = np.array(points_in)
    for order in range(1, 7):
        following = ((2 * order + 1) * points_in * current - order * previous) / (order + 1)
        previous = current
        current = following
    return current


def gll_tables():
    degree = 7
    gll_nodes = np.array(
        [
            gll_points[0],
            gll_points[1],
            gll_points[2],
            gll_points[3],
            gll_points[5],
            gll_points[6],
            gll_points[7],
            gll_points[8],
        ]
    )
    values = legendre_seven(gll_nodes)
    weights = 2.0 / (degree * (degree + 1) * values**2)
    points = degree + 1
    derivative = np.zeros((points, points))
    mass_matrix = np.zeros((points, points))
    mass_line = weights / 2.0
    for row_index in range(points):
        mass_matrix[row_index, row_index] = mass_line[row_index]
        for col_index in range(points):
            if row_index != col_index:
                derivative[row_index, col_index] = values[row_index] / (
                    values[col_index] * (gll_nodes[row_index] - gll_nodes[col_index])
                )
    derivative[0, 0] = -degree * (degree + 1) / 4.0
    derivative[degree, degree] = degree * (degree + 1) / 4.0
    stiff_line = 2.0 * derivative.T @ (weights[:, None] * derivative)
    stiffness = (
        np.kron(stiff_line, np.kron(mass_matrix, mass_matrix))
        + np.kron(mass_matrix, np.kron(stiff_line, mass_matrix))
        + np.kron(mass_matrix, np.kron(mass_matrix, stiff_line))
    )
    mass_diag = np.kron(mass_line, np.kron(mass_line, mass_line))
    return (stiffness, mass_diag, stiff_line, mass_line)


def node_weights(tiles_x, tiles_y, tiles_z):
    shared_ends = np.ones(8)
    shared_ends[0] = 2.0
    shared_ends[7] = 2.0
    vertical = np.ones((tiles_z, 8))
    vertical[1:, 0] = 2.0
    vertical[:-1, 7] = 2.0
    total = (
        shared_ends[None, :, None, None]
        * shared_ends[None, None, :, None]
        * vertical[:, None, None, :]
    )
    total = np.broadcast_to(total[None, None], (tiles_x, tiles_y, tiles_z, 8, 8, 8))
    return (1.0 / total).reshape(tiles_x * tiles_y * tiles_z, 512)


def lattice_masks():
    rows = lax.broadcasted_iota(jnp.int32, (TX * TY * TZ, 512), 0)
    lanes = lax.broadcasted_iota(jnp.int32, (TX * TY * TZ, 512), 1)
    layer = rows % TZ
    column = (rows // TZ) % TY
    node_x, node_y, node_z = lanes // 64, (lanes // 8) % 8, lanes % 8
    return {
        "z_up": (node_z == 7) & (layer < TZ - 1),
        "z_down": (node_z == 0) & (layer > 0),
        "x_up": (node_x == 7) & (rows < TY * TZ),
        "x_down": (node_x == 0) & (rows >= TY * TZ),
        "y_up": (node_y == 7) & (column == 0),
        "y_down": (node_y == 0) & (column == 1),
    }


def share_weights():
    rows = lax.broadcasted_iota(jnp.int32, (TX * TY * TZ, 512), 0)
    lanes = lax.broadcasted_iota(jnp.int32, (TX * TY * TZ, 512), 1)
    layer = rows % TZ
    node_x, node_y, node_z = lanes // 64, (lanes // 8) % 8, lanes % 8
    half = jnp.float32(0.5)
    one = jnp.float32(1.0)
    edge_x = jnp.where((node_x == 0) | (node_x == 7), half, one)
    edge_y = jnp.where((node_y == 0) | (node_y == 7), half, one)
    inner_z = ((node_z == 0) & (layer > 0)) | ((node_z == 7) & (layer < TZ - 1))
    edge_z = jnp.where(inner_z, half, one)
    return edge_x * edge_y * edge_z


def stiffness_from_lines(stiff_line, mass_line):
    line = jnp.asarray(stiff_line, jnp.float32)
    mass = jnp.eye(8, dtype=jnp.float32) * jnp.asarray(mass_line, jnp.float32)[None, :]

    def kron3(first, second, third):
        return jnp.einsum("ab,cd,ef->acebdf", first, second, third).reshape(512, 512)

    return kron3(line, mass, mass) + kron3(mass, line, mass) + kron3(mass, mass, line)


def shifted(cells, rows, lanes):
    return jnp.roll(jnp.roll(cells, -rows, axis=1), -lanes, axis=2)


def exchange(face, axis, step):
    count = lax.axis_size(axis)
    return lax.ppermute(face, axis, [(i, (i + step) % count) for i in range(count)])


def assemble(stacked):
    masks = lattice_masks()
    zero = jnp.zeros((), stacked.dtype)
    half = TY * TZ
    cells = stacked
    cells = (
        cells
        + jnp.where(masks["z_up"], shifted(cells, 1, -7), zero)
        + jnp.where(masks["z_down"], shifted(cells, -1, 7), zero)
    )
    upper = cells[:, half:, 448:]
    lower = cells[:, :half, :64]
    from_prev = exchange(upper, "stream", 1)
    from_next = exchange(lower, "stream", -1)
    inner_x = jnp.where(masks["x_up"], shifted(cells, half, -448), zero) + jnp.where(
        masks["x_down"], shifted(cells, -half, 448), zero
    )
    cells = (
        cells
        + inner_x
        + jnp.pad(from_prev, ((0, 0), (0, half), (0, 448)))
        + jnp.pad(from_next, ((0, 0), (half, 0), (448, 0)))
    )
    count = stacked.shape[0]
    sheet = cells.reshape(count, TX, TY, TZ, 8, 8, 8)
    top = sheet[:, :, 1, :, :, 7, :]
    bottom = sheet[:, :, 0, :, :, 0, :]
    top_in = exchange(top, "span", 1)
    bottom_in = exchange(bottom, "span", -1)
    inner_y = jnp.where(masks["y_up"], shifted(cells, TZ, -56), zero) + jnp.where(
        masks["y_down"], shifted(cells, -TZ, 56), zero
    )
    pads_bottom = ((0, 0), (0, 0), (0, 1), (0, 0), (0, 0), (0, 7), (0, 0))
    pads_top = ((0, 0), (0, 0), (1, 0), (0, 0), (0, 0), (7, 0), (0, 0))
    place_bottom = jnp.pad(top_in[:, :, None, :, :, None, :], pads_bottom)
    place_top = jnp.pad(bottom_in[:, :, None, :, :, None, :], pads_top)
    outside = (place_bottom + place_top).reshape(cells.shape)
    return cells + inner_y + outside


def moved(value, axis, stride, count, shift):
    size = lax.axis_size(axis)
    pairs = []
    for index in range(size):
        spot = (index // stride) % count
        pairs.append((index, index + ((spot + shift) % count - spot) * stride))
    return lax.ppermute(value, axis, pairs)


def group_sum(value, axis, stride, count):
    total, width, windows = value, 1, {1: value}
    while width * 2 <= count:
        total = total + moved(total, axis, stride, count, width)
        width *= 2
        windows[width] = total
    rest, shift = count - width, width
    for size in sorted(windows, reverse=True):
        if rest >= size:
            total = total + moved(windows[size], axis, stride, count, shift)
            shift += size
            rest -= size
    return total


def global_sum(value):
    streams = lax.axis_size("stream")
    if streams % 16 == 0:
        groups = ((1, 2), (2, 8), (16, streams // 16))
    else:
        groups = ((1, streams),)
    for stride, count in groups:
        if count > 1:
            value = group_sum(value, "stream", stride, count)
    return group_sum(value, "span", 1, lax.axis_size("span"))


def shards(right_side, conductance, element_slot):
    stiff_np, mass_np, stiff_line, mass_line = gll_tables()
    stiffness = stiffness_from_lines(stiff_line, mass_line)
    mass_diag = jnp.asarray(mass_np, jnp.float32)
    weights = share_weights()
    slot_index = element_slot[0, 0]
    picks = (slot_index[:, None] == jnp.arange(slot_index.shape[0])[None, :]).astype(jnp.float32)
    exact = lax.Precision.HIGHEST
    forcing = jnp.dot(picks, right_side[0, 0], precision=exact)
    kappa = jnp.dot(picks, conductance[0, 0][:, None], precision=exact)[:, 0]

    def local_dot(first_vec, second_vec):
        return jnp.sum(first_vec * second_vec * weights)

    def apply_local(field):
        return (
            kappa[:, None] * jnp.dot(field, stiffness, precision=lax.Precision.HIGHEST)
            + screening * mass_diag[None, :] * field
        )

    stiff_diag = jnp.asarray(np.diag(stiff_np), jnp.float32)
    diag_local = kappa[:, None] * stiff_diag[None, :] + screening * mass_diag[None, :]
    both = assemble(jnp.stack([mass_diag[None, :] * forcing, diag_local]))
    start_res = both[0]
    diag_field = both[1]
    start_z = start_res / diag_field
    first_local = apply_local(start_z)
    first_image = assemble(first_local[None])[0]
    scaled_image = first_image / diag_field
    second_local = apply_local(scaled_image)
    lane_sums = jnp.stack(
        [
            jnp.sum(start_res * start_z * weights, axis=0),
            jnp.sum(start_z * first_local, axis=0),
            jnp.sum(start_res * scaled_image * weights, axis=0),
            jnp.sum(first_image * scaled_image * weights, axis=0),
            jnp.sum(start_z * second_local, axis=0),
            jnp.sum(scaled_image * second_local, axis=0),
        ]
    )
    span = lane_sums.shape[1] // 2
    while span >= 1:
        lane_sums = lane_sums + jnp.roll(lane_sums, span, axis=1)
        span //= 2
    sums = global_sum(lane_sums)
    second_image = assemble(second_local[None])[0]
    s_rz, s_zq, s_rw, s_qw, s_zp, s_wp = (sums[n] for n in range(6))
    alpha0 = s_rz / s_zq
    rz1 = s_rz - alpha0 * (s_rw + s_zq) + alpha0 * alpha0 * s_qw
    beta = rz1 / s_rz
    grow = 1.0 + beta
    dad1 = grow * grow * s_zq - alpha0 * grow * (s_zp + s_qw) + alpha0 * alpha0 * s_wp
    alpha1 = rz1 / dad1
    alpha0, grow, alpha1 = alpha0[None, :], grow[None, :], alpha1[None, :]
    direction = grow * start_z - alpha0 * scaled_image
    image = grow * first_image - alpha0 * second_image
    solution = alpha0 * start_z + alpha1 * direction
    residual = (start_res - alpha0 * first_image) - alpha1 * image
    both_out = jnp.dot(picks.T, jnp.concatenate([solution, residual], axis=1), precision=exact)
    solution_out = both_out[:, : solution.shape[1]]
    residual_out = both_out[:, solution.shape[1] :]
    return (solution_out[None, None], residual_out[None, None])


def solution(mesh):
    placed = (P("stream", "span", None, None), P("stream", "span", None), P("stream", "span", None))
    return jax.shard_map(
        shards,
        mesh=mesh,
        in_specs=placed,
        out_specs=(P("stream", "span", None, None), P("stream", "span", None, None)),
        check_vma=False,
    )
```

```python
import jax
import jax.numpy as jnp
import numpy as np
from jax import lax
from jax.sharding import PartitionSpec as P

TX = 2
TY = 2
TZ = 24

screening = 0.1
gll_points = [
    -1.0,
    -0.8717401485096066,
    -0.5917001814331423,
    -0.2092992179024789,
    0.0,
    0.2092992179024789,
    0.5917001814331423,
    0.8717401485096066,
    1.0,
]


def legendre_seven(points_in):
    previous = np.ones(points_in.shape)
    current = np.array(points_in)
    for order in range(1, 7):
        following = ((2 * order + 1) * points_in * current - order * previous) / (order + 1)
        previous = current
        current = following
    return current


def gll_tables():
    degree = 7
    gll_nodes = np.array(
        [
            gll_points[0],
            gll_points[1],
            gll_points[2],
            gll_points[3],
            gll_points[5],
            gll_points[6],
            gll_points[7],
            gll_points[8],
        ]
    )
    values = legendre_seven(gll_nodes)
    weights = 2.0 / (degree * (degree + 1) * values**2)
    points = degree + 1
    derivative = np.zeros((points, points))
    mass_matrix = np.zeros((points, points))
    mass_line = weights / 2.0
    for row_index in range(points):
        mass_matrix[row_index, row_index] = mass_line[row_index]
        for col_index in range(points):
            if row_index != col_index:
                derivative[row_index, col_index] = values[row_index] / (
                    values[col_index] * (gll_nodes[row_index] - gll_nodes[col_index])
                )
    derivative[0, 0] = -degree * (degree + 1) / 4.0
    derivative[degree, degree] = degree * (degree + 1) / 4.0
    stiff_line = 2.0 * derivative.T @ (weights[:, None] * derivative)
    stiffness = (
        np.kron(stiff_line, np.kron(mass_matrix, mass_matrix))
        + np.kron(mass_matrix, np.kron(stiff_line, mass_matrix))
        + np.kron(mass_matrix, np.kron(mass_matrix, stiff_line))
    )
    mass_diag = np.kron(mass_line, np.kron(mass_line, mass_line))
    return (stiffness, mass_diag)


def node_weights(tiles_x, tiles_y, tiles_z):
    shared_ends = np.ones(8)
    shared_ends[0] = 2.0
    shared_ends[7] = 2.0
    vertical = np.ones((tiles_z, 8))
    vertical[1:, 0] = 2.0
    vertical[:-1, 7] = 2.0
    total = (
        shared_ends[None, :, None, None]
        * shared_ends[None, None, :, None]
        * vertical[:, None, None, :]
    )
    total = np.broadcast_to(total[None, None], (tiles_x, tiles_y, tiles_z, 8, 8, 8))
    return (1.0 / total).reshape(tiles_x * tiles_y * tiles_z, 512)


def lattice_masks():
    rows = lax.broadcasted_iota(jnp.int32, (TX * TY * TZ, 512), 0)
    lanes = lax.broadcasted_iota(jnp.int32, (TX * TY * TZ, 512), 1)
    layer = rows % TZ
    column = (rows // TZ) % TY
    node_x, node_y, node_z = lanes // 64, (lanes // 8) % 8, lanes % 8
    return {
        "z_up": (node_z == 7) & (layer < TZ - 1),
        "z_down": (node_z == 0) & (layer > 0),
        "x_up": (node_x == 7) & (rows < TY * TZ),
        "x_down": (node_x == 0) & (rows >= TY * TZ),
        "y_up": (node_y == 7) & (column == 0),
        "y_down": (node_y == 0) & (column == 1),
    }


def share_weights():
    rows = lax.broadcasted_iota(jnp.int32, (TX * TY * TZ, 512), 0)
    lanes = lax.broadcasted_iota(jnp.int32, (TX * TY * TZ, 512), 1)
    layer = rows % TZ
    node_x, node_y, node_z = lanes // 64, (lanes // 8) % 8, lanes % 8
    half = jnp.float32(0.5)
    one = jnp.float32(1.0)
    edge_x = jnp.where((node_x == 0) | (node_x == 7), half, one)
    edge_y = jnp.where((node_y == 0) | (node_y == 7), half, one)
    inner_z = ((node_z == 0) & (layer > 0)) | ((node_z == 7) & (layer < TZ - 1))
    edge_z = jnp.where(inner_z, half, one)
    return edge_x * edge_y * edge_z


def shifted(cells, rows, lanes):
    return jnp.roll(jnp.roll(cells, -rows, axis=1), -lanes, axis=2)


def exchange(face, axis, step):
    count = lax.axis_size(axis)
    return lax.ppermute(face, axis, [(i, (i + step) % count) for i in range(count)])


def assemble(stacked):
    masks = lattice_masks()
    zero = jnp.zeros((), stacked.dtype)
    half = TY * TZ
    cells = stacked
    cells = (
        cells
        + jnp.where(masks["z_up"], shifted(cells, 1, -7), zero)
        + jnp.where(masks["z_down"], shifted(cells, -1, 7), zero)
    )
    upper = cells[:, half:, 448:]
    lower = cells[:, :half, :64]
    from_prev = exchange(upper, "stream", 1)
    from_next = exchange(lower, "stream", -1)
    inner_x = jnp.where(masks["x_up"], shifted(cells, half, -448), zero) + jnp.where(
        masks["x_down"], shifted(cells, -half, 448), zero
    )
    cells = (
        cells
        + inner_x
        + jnp.pad(from_prev, ((0, 0), (0, half), (0, 448)))
        + jnp.pad(from_next, ((0, 0), (half, 0), (448, 0)))
    )
    count = stacked.shape[0]
    sheet = cells.reshape(count, TX, TY, TZ, 8, 8, 8)
    top = sheet[:, :, 1, :, :, 7, :]
    bottom = sheet[:, :, 0, :, :, 0, :]
    top_in = exchange(top, "span", 1)
    bottom_in = exchange(bottom, "span", -1)
    inner_y = jnp.where(masks["y_up"], shifted(cells, TZ, -56), zero) + jnp.where(
        masks["y_down"], shifted(cells, -TZ, 56), zero
    )
    pads_bottom = ((0, 0), (0, 0), (0, 1), (0, 0), (0, 0), (0, 7), (0, 0))
    pads_top = ((0, 0), (0, 0), (1, 0), (0, 0), (0, 0), (7, 0), (0, 0))
    place_bottom = jnp.pad(top_in[:, :, None, :, :, None, :], pads_bottom)
    place_top = jnp.pad(bottom_in[:, :, None, :, :, None, :], pads_top)
    outside = (place_bottom + place_top).reshape(cells.shape)
    return cells + inner_y + outside


def moved(value, axis, stride, count, shift):
    size = lax.axis_size(axis)
    pairs = []
    for index in range(size):
        spot = (index // stride) % count
        pairs.append((index, index + ((spot + shift) % count - spot) * stride))
    return lax.ppermute(value, axis, pairs)


def group_sum(value, axis, stride, count):
    total, width, windows = value, 1, {1: value}
    while width * 2 <= count:
        total = total + moved(total, axis, stride, count, width)
        width *= 2
        windows[width] = total
    rest, shift = count - width, width
    for size in sorted(windows, reverse=True):
        if rest >= size:
            total = total + moved(windows[size], axis, stride, count, shift)
            shift += size
            rest -= size
    return total


def global_sum(value):
    streams = lax.axis_size("stream")
    if streams % 16 == 0:
        groups = ((1, 2), (2, 8), (16, streams // 16))
    else:
        groups = ((1, streams),)
    for stride, count in groups:
        if count > 1:
            value = group_sum(value, "stream", stride, count)
    return group_sum(value, "span", 1, lax.axis_size("span"))


def shards(right_side, conductance, element_slot):
    stiff_np, mass_np = gll_tables()
    stiffness = jnp.asarray(stiff_np, jnp.float32)
    mass_diag = jnp.asarray(mass_np, jnp.float32)
    weights = share_weights()
    slot_index = element_slot[0, 0]
    picks = (slot_index[:, None] == jnp.arange(slot_index.shape[0])[None, :]).astype(jnp.float32)
    exact = lax.Precision.HIGHEST
    forcing = jnp.dot(picks, right_side[0, 0], precision=exact)
    kappa = jnp.dot(picks, conductance[0, 0][:, None], precision=exact)[:, 0]

    def local_dot(first_vec, second_vec):
        return jnp.sum(first_vec * second_vec * weights)

    def apply_local(field):
        return (
            kappa[:, None] * jnp.dot(field, stiffness, precision=lax.Precision.HIGHEST)
            + screening * mass_diag[None, :] * field
        )

    stiff_diag = jnp.asarray(np.diag(stiff_np), jnp.float32)
    diag_local = kappa[:, None] * stiff_diag[None, :] + screening * mass_diag[None, :]
    both = assemble(jnp.stack([mass_diag[None, :] * forcing, diag_local]))
    start_res = both[0]
    diag_field = both[1]
    start_z = start_res / diag_field
    first_local = apply_local(start_z)
    first_image = assemble(first_local[None])[0]
    scaled_image = first_image / diag_field
    second_local = apply_local(scaled_image)
    lane_sums = jnp.stack(
        [
            jnp.sum(start_res * start_z * weights, axis=0),
            jnp.sum(start_z * first_local, axis=0),
            jnp.sum(start_res * scaled_image * weights, axis=0),
            jnp.sum(first_image * scaled_image * weights, axis=0),
            jnp.sum(start_z * second_local, axis=0),
            jnp.sum(scaled_image * second_local, axis=0),
        ]
    )
    span = lane_sums.shape[1] // 2
    while span >= 1:
        lane_sums = lane_sums + jnp.roll(lane_sums, span, axis=1)
        span //= 2
    sums = global_sum(lane_sums)
    second_image = assemble(second_local[None])[0]
    s_rz, s_zq, s_rw, s_qw, s_zp, s_wp = (sums[n] for n in range(6))
    alpha0 = s_rz / s_zq
    rz1 = s_rz - alpha0 * (s_rw + s_zq) + alpha0 * alpha0 * s_qw
    beta = rz1 / s_rz
    grow = 1.0 + beta
    dad1 = grow * grow * s_zq - alpha0 * grow * (s_zp + s_qw) + alpha0 * alpha0 * s_wp
    alpha1 = rz1 / dad1
    alpha0, grow, alpha1 = alpha0[None, :], grow[None, :], alpha1[None, :]
    direction = grow * start_z - alpha0 * scaled_image
    image = grow * first_image - alpha0 * second_image
    solution = alpha0 * start_z + alpha1 * direction
    residual = (start_res - alpha0 * first_image) - alpha1 * image
    both_out = jnp.dot(picks.T, jnp.concatenate([solution, residual], axis=1), precision=exact)
    solution_out = both_out[:, : solution.shape[1]]
    residual_out = both_out[:, solution.shape[1] :]
    return (solution_out[None, None], residual_out[None, None])


def solution(mesh):
    placed = (P("stream", "span", None, None), P("stream", "span", None), P("stream", "span", None))
    return jax.shard_map(
        shards,
        mesh=mesh,
        in_specs=placed,
        out_specs=(P("stream", "span", None, None), P("stream", "span", None, None)),
        check_vma=False,
    )
```

```python
import jax
import jax.numpy as jnp
import numpy as np
from jax import lax
from jax.sharding import PartitionSpec as P

TX = 2
TY = 2
TZ = 24

screening = 0.1
gll_points = [
    -1.0,
    -0.8717401485096066,
    -0.5917001814331423,
    -0.2092992179024789,
    0.0,
    0.2092992179024789,
    0.5917001814331423,
    0.8717401485096066,
    1.0,
]


def legendre_seven(points_in):
    previous = np.ones(points_in.shape)
    current = np.array(points_in)
    for order in range(1, 7):
        following = ((2 * order + 1) * points_in * current - order * previous) / (order + 1)
        previous = current
        current = following
    return current


def gll_tables():
    degree = 7
    gll_nodes = np.array(
        [
            gll_points[0],
            gll_points[1],
            gll_points[2],
            gll_points[3],
            gll_points[5],
            gll_points[6],
            gll_points[7],
            gll_points[8],
        ]
    )
    values = legendre_seven(gll_nodes)
    weights = 2.0 / (degree * (degree + 1) * values**2)
    points = degree + 1
    derivative = np.zeros((points, points))
    mass_matrix = np.zeros((points, points))
    mass_line = weights / 2.0
    for row_index in range(points):
        mass_matrix[row_index, row_index] = mass_line[row_index]
        for col_index in range(points):
            if row_index != col_index:
                derivative[row_index, col_index] = values[row_index] / (
                    values[col_index] * (gll_nodes[row_index] - gll_nodes[col_index])
                )
    derivative[0, 0] = -degree * (degree + 1) / 4.0
    derivative[degree, degree] = degree * (degree + 1) / 4.0
    stiff_line = 2.0 * derivative.T @ (weights[:, None] * derivative)
    stiffness = (
        np.kron(stiff_line, np.kron(mass_matrix, mass_matrix))
        + np.kron(mass_matrix, np.kron(stiff_line, mass_matrix))
        + np.kron(mass_matrix, np.kron(mass_matrix, stiff_line))
    )
    mass_diag = np.kron(mass_line, np.kron(mass_line, mass_line))
    return (stiffness, mass_diag)


def node_weights(tiles_x, tiles_y, tiles_z):
    shared_ends = np.ones(8)
    shared_ends[0] = 2.0
    shared_ends[7] = 2.0
    vertical = np.ones((tiles_z, 8))
    vertical[1:, 0] = 2.0
    vertical[:-1, 7] = 2.0
    total = (
        shared_ends[None, :, None, None]
        * shared_ends[None, None, :, None]
        * vertical[:, None, None, :]
    )
    total = np.broadcast_to(total[None, None], (tiles_x, tiles_y, tiles_z, 8, 8, 8))
    return (1.0 / total).reshape(tiles_x * tiles_y * tiles_z, 512)


def lattice_masks():
    rows = lax.broadcasted_iota(jnp.int32, (TX * TY * TZ, 512), 0)
    lanes = lax.broadcasted_iota(jnp.int32, (TX * TY * TZ, 512), 1)
    layer = rows % TZ
    column = (rows // TZ) % TY
    node_x, node_y, node_z = lanes // 64, (lanes // 8) % 8, lanes % 8
    return {
        "z_up": (node_z == 7) & (layer < TZ - 1),
        "z_down": (node_z == 0) & (layer > 0),
        "x_up": (node_x == 7) & (rows < TY * TZ),
        "x_down": (node_x == 0) & (rows >= TY * TZ),
        "y_up": (node_y == 7) & (column == 0),
        "y_down": (node_y == 0) & (column == 1),
    }


def share_weights():
    rows = lax.broadcasted_iota(jnp.int32, (TX * TY * TZ, 512), 0)
    lanes = lax.broadcasted_iota(jnp.int32, (TX * TY * TZ, 512), 1)
    layer = rows % TZ
    node_x, node_y, node_z = lanes // 64, (lanes // 8) % 8, lanes % 8
    half = jnp.float32(0.5)
    one = jnp.float32(1.0)
    edge_x = jnp.where((node_x == 0) | (node_x == 7), half, one)
    edge_y = jnp.where((node_y == 0) | (node_y == 7), half, one)
    inner_z = ((node_z == 0) & (layer > 0)) | ((node_z == 7) & (layer < TZ - 1))
    edge_z = jnp.where(inner_z, half, one)
    return edge_x * edge_y * edge_z


def shifted(cells, rows, lanes):
    return jnp.roll(jnp.roll(cells, -rows, axis=1), -lanes, axis=2)


def exchange(face, axis, step):
    count = lax.axis_size(axis)
    return lax.ppermute(face, axis, [(i, (i + step) % count) for i in range(count)])


def face_lanes(plane):
    lanes = lax.broadcasted_iota(jnp.int32, (512, 64), 0)
    slots = lax.broadcasted_iota(jnp.int32, (512, 64), 1)
    return (lanes == (slots // 8) * 64 + plane * 8 + slots % 8).astype(jnp.float32)


def lane_dot(cells, table):
    return jnp.einsum("frn,nc->frc", cells, table, precision=lax.Precision.HIGHEST)


def assemble(stacked):
    masks = lattice_masks()
    zero = jnp.zeros((), stacked.dtype)
    half = TY * TZ
    count = stacked.shape[0]
    cells = stacked
    cells = (
        cells
        + jnp.where(masks["z_up"], shifted(cells, 1, -7), zero)
        + jnp.where(masks["z_down"], shifted(cells, -1, 7), zero)
    )
    upper = cells[:, half:, 448:]
    lower = cells[:, :half, :64]
    from_prev = exchange(upper, "stream", 1)
    from_next = exchange(lower, "stream", -1)
    inner_x = jnp.where(masks["x_up"], shifted(cells, half, -448), zero) + jnp.where(
        masks["x_down"], shifted(cells, -half, 448), zero
    )
    cells = (
        cells
        + inner_x
        + jnp.pad(from_prev, ((0, 0), (0, half), (0, 448)))
        + jnp.pad(from_next, ((0, 0), (half, 0), (448, 0)))
    )
    blocks = cells.reshape(count, TX, TY, TZ, 512)
    top_lanes = face_lanes(7)
    bottom_lanes = face_lanes(0)
    top = lane_dot(blocks[:, :, 1].reshape(count, TX * TZ, 512), top_lanes)
    bottom = lane_dot(blocks[:, :, 0].reshape(count, TX * TZ, 512), bottom_lanes)
    top_in = exchange(top, "span", 1)
    bottom_in = exchange(bottom, "span", -1)
    inner_y = jnp.where(masks["y_up"], shifted(cells, TZ, -56), zero) + jnp.where(
        masks["y_down"], shifted(cells, -TZ, 56), zero
    )
    into_bottom = lane_dot(top_in, bottom_lanes.T).reshape(count, TX, 1, TZ, 512)
    into_top = lane_dot(bottom_in, top_lanes.T).reshape(count, TX, 1, TZ, 512)
    outside = jnp.concatenate([into_bottom, into_top], axis=2).reshape(cells.shape)
    return cells + inner_y + outside


def moved(value, axis, stride, count, shift):
    size = lax.axis_size(axis)
    pairs = []
    for index in range(size):
        spot = (index // stride) % count
        pairs.append((index, index + ((spot + shift) % count - spot) * stride))
    return lax.ppermute(value, axis, pairs)


def group_sum(value, axis, stride, count):
    total, width, windows = value, 1, {1: value}
    while width * 2 <= count:
        total = total + moved(total, axis, stride, count, width)
        width *= 2
        windows[width] = total
    rest, shift = count - width, width
    for size in sorted(windows, reverse=True):
        if rest >= size:
            total = total + moved(windows[size], axis, stride, count, shift)
            shift += size
            rest -= size
    return total


def global_sum(value):
    streams = lax.axis_size("stream")
    if streams % 16 == 0:
        groups = ((1, 2), (2, 8), (16, streams // 16))
    else:
        groups = ((1, streams),)
    for stride, count in groups:
        if count > 1:
            value = group_sum(value, "stream", stride, count)
    return group_sum(value, "span", 1, lax.axis_size("span"))


def shards(right_side, conductance, element_slot):
    stiff_np, mass_np = gll_tables()
    stiffness = jnp.asarray(stiff_np, jnp.float32)
    mass_diag = jnp.asarray(mass_np, jnp.float32)
    weights = share_weights()
    slot_index = element_slot[0, 0]
    picks = (slot_index[:, None] == jnp.arange(slot_index.shape[0])[None, :]).astype(jnp.float32)
    exact = lax.Precision.HIGHEST
    forcing = jnp.dot(picks, right_side[0, 0], precision=exact)
    kappa = jnp.dot(picks, conductance[0, 0][:, None], precision=exact)[:, 0]

    def local_dot(first_vec, second_vec):
        return jnp.sum(first_vec * second_vec * weights)

    def apply_local(field):
        return (
            kappa[:, None] * jnp.dot(field, stiffness, precision=lax.Precision.HIGHEST)
            + screening * mass_diag[None, :] * field
        )

    stiff_diag = jnp.asarray(np.diag(stiff_np), jnp.float32)
    diag_local = kappa[:, None] * stiff_diag[None, :] + screening * mass_diag[None, :]
    both = assemble(jnp.stack([mass_diag[None, :] * forcing, diag_local]))
    start_res = both[0]
    diag_field = both[1]
    start_z = start_res / diag_field
    first_local = apply_local(start_z)
    first_image = assemble(first_local[None])[0]
    scaled_image = first_image / diag_field
    second_local = apply_local(scaled_image)
    lane_sums = jnp.stack(
        [
            jnp.sum(start_res * start_z * weights, axis=0),
            jnp.sum(start_z * first_local, axis=0),
            jnp.sum(start_res * scaled_image * weights, axis=0),
            jnp.sum(first_image * scaled_image * weights, axis=0),
            jnp.sum(start_z * second_local, axis=0),
            jnp.sum(scaled_image * second_local, axis=0),
        ]
    )
    span = lane_sums.shape[1] // 2
    while span >= 1:
        lane_sums = lane_sums + jnp.roll(lane_sums, span, axis=1)
        span //= 2
    sums = global_sum(lane_sums)
    second_image = assemble(second_local[None])[0]
    s_rz, s_zq, s_rw, s_qw, s_zp, s_wp = (sums[n] for n in range(6))
    alpha0 = s_rz / s_zq
    rz1 = s_rz - alpha0 * (s_rw + s_zq) + alpha0 * alpha0 * s_qw
    beta = rz1 / s_rz
    grow = 1.0 + beta
    dad1 = grow * grow * s_zq - alpha0 * grow * (s_zp + s_qw) + alpha0 * alpha0 * s_wp
    alpha1 = rz1 / dad1
    alpha0, grow, alpha1 = alpha0[None, :], grow[None, :], alpha1[None, :]
    direction = grow * start_z - alpha0 * scaled_image
    image = grow * first_image - alpha0 * second_image
    solution = alpha0 * start_z + alpha1 * direction
    residual = (start_res - alpha0 * first_image) - alpha1 * image
    both_out = jnp.dot(picks.T, jnp.concatenate([solution, residual], axis=1), precision=exact)
    solution_out = both_out[:, : solution.shape[1]]
    residual_out = both_out[:, solution.shape[1] :]
    return (solution_out[None, None], residual_out[None, None])


def solution(mesh):
    placed = (P("stream", "span", None, None), P("stream", "span", None), P("stream", "span", None))
    return jax.shard_map(
        shards,
        mesh=mesh,
        in_specs=placed,
        out_specs=(P("stream", "span", None, None), P("stream", "span", None, None)),
        check_vma=False,
    )
```

```python
import jax
import jax.numpy as jnp
import numpy as np
from jax import lax
from jax.sharding import PartitionSpec as P

TX = 2
TY = 2
TZ = 24

screening = 0.1
gll_points = [
    -1.0,
    -0.8717401485096066,
    -0.5917001814331423,
    -0.2092992179024789,
    0.0,
    0.2092992179024789,
    0.5917001814331423,
    0.8717401485096066,
    1.0,
]


def legendre_seven(points_in):
    previous = np.ones(points_in.shape)
    current = np.array(points_in)
    for order in range(1, 7):
        following = ((2 * order + 1) * points_in * current - order * previous) / (order + 1)
        previous = current
        current = following
    return current


def gll_tables():
    degree = 7
    gll_nodes = np.array(
        [
            gll_points[0],
            gll_points[1],
            gll_points[2],
            gll_points[3],
            gll_points[5],
            gll_points[6],
            gll_points[7],
            gll_points[8],
        ]
    )
    values = legendre_seven(gll_nodes)
    weights = 2.0 / (degree * (degree + 1) * values**2)
    points = degree + 1
    derivative = np.zeros((points, points))
    mass_matrix = np.zeros((points, points))
    mass_line = weights / 2.0
    for row_index in range(points):
        mass_matrix[row_index, row_index] = mass_line[row_index]
        for col_index in range(points):
            if row_index != col_index:
                derivative[row_index, col_index] = values[row_index] / (
                    values[col_index] * (gll_nodes[row_index] - gll_nodes[col_index])
                )
    derivative[0, 0] = -degree * (degree + 1) / 4.0
    derivative[degree, degree] = degree * (degree + 1) / 4.0
    stiff_line = 2.0 * derivative.T @ (weights[:, None] * derivative)
    stiffness = (
        np.kron(stiff_line, np.kron(mass_matrix, mass_matrix))
        + np.kron(mass_matrix, np.kron(stiff_line, mass_matrix))
        + np.kron(mass_matrix, np.kron(mass_matrix, stiff_line))
    )
    mass_diag = np.kron(mass_line, np.kron(mass_line, mass_line))
    return (stiffness, mass_diag)


def node_weights(tiles_x, tiles_y, tiles_z):
    shared_ends = np.ones(8)
    shared_ends[0] = 2.0
    shared_ends[7] = 2.0
    vertical = np.ones((tiles_z, 8))
    vertical[1:, 0] = 2.0
    vertical[:-1, 7] = 2.0
    total = (
        shared_ends[None, :, None, None]
        * shared_ends[None, None, :, None]
        * vertical[:, None, None, :]
    )
    total = np.broadcast_to(total[None, None], (tiles_x, tiles_y, tiles_z, 8, 8, 8))
    return (1.0 / total).reshape(tiles_x * tiles_y * tiles_z, 512)


def lattice_masks():
    rows = lax.broadcasted_iota(jnp.int32, (TX * TY * TZ, 512), 0)
    lanes = lax.broadcasted_iota(jnp.int32, (TX * TY * TZ, 512), 1)
    layer = rows % TZ
    column = (rows // TZ) % TY
    node_x, node_y, node_z = lanes // 64, (lanes // 8) % 8, lanes % 8
    return {
        "z_up": (node_z == 7) & (layer < TZ - 1),
        "z_down": (node_z == 0) & (layer > 0),
        "x_up": (node_x == 7) & (rows < TY * TZ),
        "x_down": (node_x == 0) & (rows >= TY * TZ),
        "y_up": (node_y == 7) & (column == 0),
        "y_down": (node_y == 0) & (column == 1),
    }


def share_weights():
    rows = lax.broadcasted_iota(jnp.int32, (TX * TY * TZ, 512), 0)
    lanes = lax.broadcasted_iota(jnp.int32, (TX * TY * TZ, 512), 1)
    layer = rows % TZ
    node_x, node_y, node_z = lanes // 64, (lanes // 8) % 8, lanes % 8
    half = jnp.float32(0.5)
    one = jnp.float32(1.0)
    edge_x = jnp.where((node_x == 0) | (node_x == 7), half, one)
    edge_y = jnp.where((node_y == 0) | (node_y == 7), half, one)
    inner_z = ((node_z == 0) & (layer > 0)) | ((node_z == 7) & (layer < TZ - 1))
    edge_z = jnp.where(inner_z, half, one)
    return edge_x * edge_y * edge_z


def shifted(cells, rows, lanes):
    return jnp.roll(jnp.roll(cells, -rows, axis=1), -lanes, axis=2)


def exchange(face, axis, step):
    count = lax.axis_size(axis)
    return lax.ppermute(face, axis, [(i, (i + step) % count) for i in range(count)])


def face_lanes(plane):
    lanes = lax.broadcasted_iota(jnp.int32, (512, 64), 0)
    slots = lax.broadcasted_iota(jnp.int32, (512, 64), 1)
    return (lanes == (slots // 8) * 64 + plane * 8 + slots % 8).astype(jnp.float32)


def lane_dot(cells, table):
    return jnp.einsum("frn,nc->frc", cells, table, precision=lax.Precision.HIGHEST)


def assemble(stacked):
    masks = lattice_masks()
    zero = jnp.zeros((), stacked.dtype)
    half = TY * TZ
    count = stacked.shape[0]
    cells = stacked
    cells = (
        cells
        + jnp.where(masks["z_up"], shifted(cells, 1, -7), zero)
        + jnp.where(masks["z_down"], shifted(cells, -1, 7), zero)
    )
    upper = cells[:, half:, 448:]
    lower = cells[:, :half, :64]
    from_prev = exchange(upper, "stream", 1)
    from_next = exchange(lower, "stream", -1)
    inner_x = jnp.where(masks["x_up"], shifted(cells, half, -448), zero) + jnp.where(
        masks["x_down"], shifted(cells, -half, 448), zero
    )
    cells = (
        cells
        + inner_x
        + jnp.pad(from_prev, ((0, 0), (0, half), (0, 448)))
        + jnp.pad(from_next, ((0, 0), (half, 0), (448, 0)))
    )
    blocks = cells.reshape(count, TX, TY, TZ, 512)
    top_lanes = face_lanes(7)
    bottom_lanes = face_lanes(0)
    top = lane_dot(blocks[:, :, 1].reshape(count, TX * TZ, 512), top_lanes)
    bottom = lane_dot(blocks[:, :, 0].reshape(count, TX * TZ, 512), bottom_lanes)
    top_in = exchange(top, "span", 1)
    bottom_in = exchange(bottom, "span", -1)
    inner_y = jnp.where(masks["y_up"], shifted(cells, TZ, -56), zero) + jnp.where(
        masks["y_down"], shifted(cells, -TZ, 56), zero
    )
    into_bottom = lane_dot(top_in, bottom_lanes.T).reshape(count, TX, 1, TZ, 512)
    into_top = lane_dot(bottom_in, top_lanes.T).reshape(count, TX, 1, TZ, 512)
    outside = jnp.concatenate([into_bottom, into_top], axis=2).reshape(cells.shape)
    return cells + inner_y + outside


def moved(value, axis, stride, count, shift):
    size = lax.axis_size(axis)
    pairs = []
    for index in range(size):
        spot = (index // stride) % count
        pairs.append((index, index + ((spot + shift) % count - spot) * stride))
    return lax.ppermute(value, axis, pairs)


def group_sum(value, axis, stride, count):
    total, width, windows = value, 1, {1: value}
    while width * 2 <= count:
        total = total + moved(total, axis, stride, count, width)
        width *= 2
        windows[width] = total
    rest, shift = count - width, width
    for size in sorted(windows, reverse=True):
        if rest >= size:
            total = total + moved(windows[size], axis, stride, count, shift)
            shift += size
            rest -= size
    return total


def global_sum(value):
    streams = lax.axis_size("stream")
    if streams % 16 == 0:
        groups = ((1, 2), (2, 8), (16, streams // 16))
    else:
        groups = ((1, streams),)
    for stride, count in groups:
        if count > 1:
            value = group_sum(value, "stream", stride, count)
    return group_sum(value, "span", 1, lax.axis_size("span"))


def assemble_with_sum(stacked, lane_sums):
    masks = lattice_masks()
    zero = jnp.zeros((), stacked.dtype)
    half = TY * TZ
    count = stacked.shape[0]
    partial = lane_sums[:, :64]
    cells = stacked
    cells = (
        cells
        + jnp.where(masks["z_up"], shifted(cells, 1, -7), zero)
        + jnp.where(masks["z_down"], shifted(cells, -1, 7), zero)
    )
    upper = jnp.concatenate([cells[0, half:, 448:], partial], axis=0)
    lower = jnp.concatenate([cells[0, :half, :64], partial], axis=0)
    got_prev = exchange(upper, "stream", 1)
    got_next = exchange(lower, "stream", -1)
    from_prev, from_next = got_prev[None, :half], got_next[None, :half]
    odd = lax.axis_index("stream") % 2 == 1
    partial = partial + jnp.where(odd, got_prev[half:], got_next[half:])
    inner_x = jnp.where(masks["x_up"], shifted(cells, half, -448), zero) + jnp.where(
        masks["x_down"], shifted(cells, -half, 448), zero
    )
    cells = (
        cells
        + inner_x
        + jnp.pad(from_prev, ((0, 0), (0, half), (0, 448)))
        + jnp.pad(from_next, ((0, 0), (half, 0), (448, 0)))
    )
    blocks = cells.reshape(count, TX, TY, TZ, 512)
    top_lanes = face_lanes(7)
    bottom_lanes = face_lanes(0)
    top = lane_dot(blocks[:, :, 1].reshape(count, TX * TZ, 512), top_lanes)
    bottom = lane_dot(blocks[:, :, 0].reshape(count, TX * TZ, 512), bottom_lanes)
    got_top = exchange(jnp.concatenate([top[0], partial], axis=0), "span", 1)
    got_bottom = exchange(jnp.concatenate([bottom[0], partial], axis=0), "span", -1)
    top_in, bottom_in = got_top[None, :half], got_bottom[None, :half]
    partial = partial + got_top[half:] + got_bottom[half:]
    inner_y = jnp.where(masks["y_up"], shifted(cells, TZ, -56), zero) + jnp.where(
        masks["y_down"], shifted(cells, -TZ, 56), zero
    )
    into_bottom = lane_dot(top_in, bottom_lanes.T).reshape(count, TX, 1, TZ, 512)
    into_top = lane_dot(bottom_in, top_lanes.T).reshape(count, TX, 1, TZ, 512)
    outside = jnp.concatenate([into_bottom, into_top], axis=2).reshape(cells.shape)
    streams = lax.axis_size("stream")
    if streams % 16 == 0:
        groups = ((2, 8), (16, streams // 16))
    else:
        groups = ((2, streams // 2),)
    for stride, size in groups:
        if size > 1:
            partial = group_sum(partial, "stream", stride, size)
    partial = unit_sum(partial, "span", 3, lax.axis_size("span") // 3)
    return cells + inner_y + outside, jnp.tile(partial, (1, 8))


def unit_sum(value, axis, unit, units):
    total, width, windows = value, 1, {1: value}
    while width * 2 <= units:
        total = total + moved(total, axis, 1, unit * units, width * unit)
        width *= 2
        windows[width] = total
    rest, shift = units - width, width
    for size in sorted(windows, reverse=True):
        if rest >= size:
            total = total + moved(windows[size], axis, 1, unit * units, shift * unit)
            shift += size
            rest -= size
    return total


def shards(right_side, conductance, element_slot):
    stiff_np, mass_np = gll_tables()
    stiffness = jnp.asarray(stiff_np, jnp.float32)
    mass_diag = jnp.asarray(mass_np, jnp.float32)
    weights = share_weights()
    slot_index = element_slot[0, 0]
    picks = (slot_index[:, None] == jnp.arange(slot_index.shape[0])[None, :]).astype(jnp.float32)
    exact = lax.Precision.HIGHEST
    forcing = jnp.dot(picks, right_side[0, 0], precision=exact)
    kappa = jnp.dot(picks, conductance[0, 0][:, None], precision=exact)[:, 0]

    def local_dot(first_vec, second_vec):
        return jnp.sum(first_vec * second_vec * weights)

    def apply_local(field):
        return (
            kappa[:, None] * jnp.dot(field, stiffness, precision=lax.Precision.HIGHEST)
            + screening * mass_diag[None, :] * field
        )

    stiff_diag = jnp.asarray(np.diag(stiff_np), jnp.float32)
    diag_local = kappa[:, None] * stiff_diag[None, :] + screening * mass_diag[None, :]
    both = assemble(jnp.stack([mass_diag[None, :] * forcing, diag_local]))
    start_res = both[0]
    diag_field = both[1]
    start_z = start_res / diag_field
    first_local = apply_local(start_z)
    first_image = assemble(first_local[None])[0]
    scaled_image = first_image / diag_field
    second_local = apply_local(scaled_image)
    lane_sums = jnp.stack(
        [
            jnp.sum(start_res * start_z * weights, axis=0),
            jnp.sum(start_z * first_local, axis=0),
            jnp.sum(start_res * scaled_image * weights, axis=0),
            jnp.sum(first_image * scaled_image * weights, axis=0),
            jnp.sum(start_z * second_local, axis=0),
            jnp.sum(scaled_image * second_local, axis=0),
        ]
    )
    span = lane_sums.shape[1] // 2
    while span >= 1:
        lane_sums = lane_sums + jnp.roll(lane_sums, span, axis=1)
        span //= 2
    second_image, sums = assemble_with_sum(second_local[None], lane_sums)
    second_image = second_image[0]
    s_rz, s_zq, s_rw, s_qw, s_zp, s_wp = (sums[n] for n in range(6))
    alpha0 = s_rz / s_zq
    rz1 = s_rz - alpha0 * (s_rw + s_zq) + alpha0 * alpha0 * s_qw
    beta = rz1 / s_rz
    grow = 1.0 + beta
    dad1 = grow * grow * s_zq - alpha0 * grow * (s_zp + s_qw) + alpha0 * alpha0 * s_wp
    alpha1 = rz1 / dad1
    alpha0, grow, alpha1 = alpha0[None, :], grow[None, :], alpha1[None, :]
    direction = grow * start_z - alpha0 * scaled_image
    image = grow * first_image - alpha0 * second_image
    solution = alpha0 * start_z + alpha1 * direction
    residual = (start_res - alpha0 * first_image) - alpha1 * image
    both_out = jnp.dot(picks.T, jnp.concatenate([solution, residual], axis=1), precision=exact)
    solution_out = both_out[:, : solution.shape[1]]
    residual_out = both_out[:, solution.shape[1] :]
    return (solution_out[None, None], residual_out[None, None])


def solution(mesh):
    placed = (P("stream", "span", None, None), P("stream", "span", None), P("stream", "span", None))
    return jax.shard_map(
        shards,
        mesh=mesh,
        in_specs=placed,
        out_specs=(P("stream", "span", None, None), P("stream", "span", None, None)),
        check_vma=False,
    )
```

```python
import jax
import jax.numpy as jnp
import numpy as np
from jax import lax
from jax.sharding import PartitionSpec as P

TX = 2
TY = 2
TZ = 24

screening = 0.1
gll_points = [
    -1.0,
    -0.8717401485096066,
    -0.5917001814331423,
    -0.2092992179024789,
    0.0,
    0.2092992179024789,
    0.5917001814331423,
    0.8717401485096066,
    1.0,
]


def legendre_seven(points_in):
    previous = np.ones(points_in.shape)
    current = np.array(points_in)
    for order in range(1, 7):
        following = ((2 * order + 1) * points_in * current - order * previous) / (order + 1)
        previous = current
        current = following
    return current


def gll_tables():
    degree = 7
    gll_nodes = np.array(
        [
            gll_points[0],
            gll_points[1],
            gll_points[2],
            gll_points[3],
            gll_points[5],
            gll_points[6],
            gll_points[7],
            gll_points[8],
        ]
    )
    values = legendre_seven(gll_nodes)
    weights = 2.0 / (degree * (degree + 1) * values**2)
    points = degree + 1
    derivative = np.zeros((points, points))
    mass_matrix = np.zeros((points, points))
    mass_line = weights / 2.0
    for row_index in range(points):
        mass_matrix[row_index, row_index] = mass_line[row_index]
        for col_index in range(points):
            if row_index != col_index:
                derivative[row_index, col_index] = values[row_index] / (
                    values[col_index] * (gll_nodes[row_index] - gll_nodes[col_index])
                )
    derivative[0, 0] = -degree * (degree + 1) / 4.0
    derivative[degree, degree] = degree * (degree + 1) / 4.0
    stiff_line = 2.0 * derivative.T @ (weights[:, None] * derivative)
    stiffness = (
        np.kron(stiff_line, np.kron(mass_matrix, mass_matrix))
        + np.kron(mass_matrix, np.kron(stiff_line, mass_matrix))
        + np.kron(mass_matrix, np.kron(mass_matrix, stiff_line))
    )
    mass_diag = np.kron(mass_line, np.kron(mass_line, mass_line))
    return (stiffness, mass_diag)


def node_weights(tiles_x, tiles_y, tiles_z):
    shared_ends = np.ones(8)
    shared_ends[0] = 2.0
    shared_ends[7] = 2.0
    vertical = np.ones((tiles_z, 8))
    vertical[1:, 0] = 2.0
    vertical[:-1, 7] = 2.0
    total = (
        shared_ends[None, :, None, None]
        * shared_ends[None, None, :, None]
        * vertical[:, None, None, :]
    )
    total = np.broadcast_to(total[None, None], (tiles_x, tiles_y, tiles_z, 8, 8, 8))
    return (1.0 / total).reshape(tiles_x * tiles_y * tiles_z, 512)


def lattice_masks():
    rows = lax.broadcasted_iota(jnp.int32, (TX * TY * TZ, 512), 0)
    lanes = lax.broadcasted_iota(jnp.int32, (TX * TY * TZ, 512), 1)
    layer = rows % TZ
    column = (rows // TZ) % TY
    node_x, node_y, node_z = lanes // 64, (lanes // 8) % 8, lanes % 8
    return {
        "z_up": (node_z == 7) & (layer < TZ - 1),
        "z_down": (node_z == 0) & (layer > 0),
        "x_up": (node_x == 7) & (rows < TY * TZ),
        "x_down": (node_x == 0) & (rows >= TY * TZ),
        "y_up": (node_y == 7) & (column == 0),
        "y_down": (node_y == 0) & (column == 1),
    }


def share_weights():
    rows = lax.broadcasted_iota(jnp.int32, (TX * TY * TZ, 512), 0)
    lanes = lax.broadcasted_iota(jnp.int32, (TX * TY * TZ, 512), 1)
    layer = rows % TZ
    node_x, node_y, node_z = lanes // 64, (lanes // 8) % 8, lanes % 8
    half = jnp.float32(0.5)
    one = jnp.float32(1.0)
    edge_x = jnp.where((node_x == 0) | (node_x == 7), half, one)
    edge_y = jnp.where((node_y == 0) | (node_y == 7), half, one)
    inner_z = ((node_z == 0) & (layer > 0)) | ((node_z == 7) & (layer < TZ - 1))
    edge_z = jnp.where(inner_z, half, one)
    return edge_x * edge_y * edge_z


def shifted(cells, rows, lanes):
    return jnp.roll(jnp.roll(cells, -rows, axis=1), -lanes, axis=2)


def exchange(face, axis, step):
    count = lax.axis_size(axis)
    return lax.ppermute(face, axis, [(i, (i + step) % count) for i in range(count)])


def swap_faces(upper, lower, axis):
    count = lax.axis_size(axis)
    if count % 2:
        return exchange(upper, axis, 1), exchange(lower, axis, -1)
    even = lax.axis_index(axis) % 2 == 0
    inner = [(i, i ^ 1) for i in range(count)]
    outer = [(i, (i + 1) % count if i % 2 else (i - 1) % count) for i in range(count)]
    got_inner = lax.ppermute(jnp.where(even, upper, lower), axis, inner)
    got_outer = lax.ppermute(jnp.where(even, lower, upper), axis, outer)
    return jnp.where(even, got_outer, got_inner), jnp.where(even, got_inner, got_outer)


def face_lanes(plane):
    lanes = lax.broadcasted_iota(jnp.int32, (512, 64), 0)
    slots = lax.broadcasted_iota(jnp.int32, (512, 64), 1)
    return (lanes == (slots // 8) * 64 + plane * 8 + slots % 8).astype(jnp.float32)


def lane_dot(cells, table):
    return jnp.einsum("frn,nc->frc", cells, table, precision=lax.Precision.HIGHEST)


def assemble(stacked):
    masks = lattice_masks()
    zero = jnp.zeros((), stacked.dtype)
    half = TY * TZ
    count = stacked.shape[0]
    cells = stacked
    cells = (
        cells
        + jnp.where(masks["z_up"], shifted(cells, 1, -7), zero)
        + jnp.where(masks["z_down"], shifted(cells, -1, 7), zero)
    )
    upper = cells[:, half:, 448:]
    lower = cells[:, :half, :64]
    from_prev, from_next = swap_faces(upper, lower, "stream")
    inner_x = jnp.where(masks["x_up"], shifted(cells, half, -448), zero) + jnp.where(
        masks["x_down"], shifted(cells, -half, 448), zero
    )
    cells = (
        cells
        + inner_x
        + jnp.pad(from_prev, ((0, 0), (0, half), (0, 448)))
        + jnp.pad(from_next, ((0, 0), (half, 0), (448, 0)))
    )
    blocks = cells.reshape(count, TX, TY, TZ, 512)
    top_lanes = face_lanes(7)
    bottom_lanes = face_lanes(0)
    top = lane_dot(blocks[:, :, 1].reshape(count, TX * TZ, 512), top_lanes)
    bottom = lane_dot(blocks[:, :, 0].reshape(count, TX * TZ, 512), bottom_lanes)
    top_in, bottom_in = swap_faces(top, bottom, "span")
    inner_y = jnp.where(masks["y_up"], shifted(cells, TZ, -56), zero) + jnp.where(
        masks["y_down"], shifted(cells, -TZ, 56), zero
    )
    into_bottom = lane_dot(top_in, bottom_lanes.T).reshape(count, TX, 1, TZ, 512)
    into_top = lane_dot(bottom_in, top_lanes.T).reshape(count, TX, 1, TZ, 512)
    outside = jnp.concatenate([into_bottom, into_top], axis=2).reshape(cells.shape)
    return cells + inner_y + outside


def moved(value, axis, stride, count, shift):
    size = lax.axis_size(axis)
    pairs = []
    for index in range(size):
        spot = (index // stride) % count
        pairs.append((index, index + ((spot + shift) % count - spot) * stride))
    return lax.ppermute(value, axis, pairs)


def group_sum(value, axis, stride, count):
    if count & (count - 1) == 0:
        size = lax.axis_size(axis)
        bit = 1
        while bit < count:
            pairs = [(i, i + ((((i // stride) % count) ^ bit) - (i // stride) % count) * stride) for i in range(size)]
            value = value + lax.ppermute(value, axis, pairs)
            bit *= 2
        return value
    total, width, windows = value, 1, {1: value}
    while width * 2 <= count:
        total = total + moved(total, axis, stride, count, width)
        width *= 2
        windows[width] = total
    rest, shift = count - width, width
    for size in sorted(windows, reverse=True):
        if rest >= size:
            total = total + moved(windows[size], axis, stride, count, shift)
            shift += size
            rest -= size
    return total


def global_sum(value):
    streams = lax.axis_size("stream")
    if streams % 16 == 0:
        groups = ((1, 2), (2, 8), (16, streams // 16))
    else:
        groups = ((1, streams),)
    for stride, count in groups:
        if count > 1:
            value = group_sum(value, "stream", stride, count)
    return group_sum(value, "span", 1, lax.axis_size("span"))


def shards(right_side, conductance, element_slot):
    stiff_np, mass_np = gll_tables()
    stiffness = jnp.asarray(stiff_np, jnp.float32)
    mass_diag = jnp.asarray(mass_np, jnp.float32)
    weights = share_weights()
    slot_index = element_slot[0, 0]
    picks = (slot_index[:, None] == jnp.arange(slot_index.shape[0])[None, :]).astype(jnp.float32)
    exact = lax.Precision.HIGHEST
    forcing = jnp.dot(picks, right_side[0, 0], precision=exact)
    kappa = jnp.dot(picks, conductance[0, 0][:, None], precision=exact)[:, 0]

    def local_dot(first_vec, second_vec):
        return jnp.sum(first_vec * second_vec * weights)

    def apply_local(field):
        return (
            kappa[:, None] * jnp.dot(field, stiffness, precision=lax.Precision.HIGHEST)
            + screening * mass_diag[None, :] * field
        )

    stiff_diag = jnp.asarray(np.diag(stiff_np), jnp.float32)
    diag_local = kappa[:, None] * stiff_diag[None, :] + screening * mass_diag[None, :]
    both = assemble(jnp.stack([mass_diag[None, :] * forcing, diag_local]))
    start_res = both[0]
    diag_field = both[1]
    start_z = start_res / diag_field
    first_local = apply_local(start_z)
    first_image = assemble(first_local[None])[0]
    scaled_image = first_image / diag_field
    second_local = apply_local(scaled_image)
    lane_sums = jnp.stack(
        [
            jnp.sum(start_res * start_z * weights, axis=0),
            jnp.sum(start_z * first_local, axis=0),
            jnp.sum(start_res * scaled_image * weights, axis=0),
            jnp.sum(first_image * scaled_image * weights, axis=0),
            jnp.sum(start_z * second_local, axis=0),
            jnp.sum(scaled_image * second_local, axis=0),
        ]
    )
    span = lane_sums.shape[1] // 2
    while span >= 1:
        lane_sums = lane_sums + jnp.roll(lane_sums, span, axis=1)
        span //= 2
    sums = global_sum(lane_sums)
    second_image = assemble(second_local[None])[0]
    s_rz, s_zq, s_rw, s_qw, s_zp, s_wp = (sums[n] for n in range(6))
    alpha0 = s_rz / s_zq
    rz1 = s_rz - alpha0 * (s_rw + s_zq) + alpha0 * alpha0 * s_qw
    beta = rz1 / s_rz
    grow = 1.0 + beta
    dad1 = grow * grow * s_zq - alpha0 * grow * (s_zp + s_qw) + alpha0 * alpha0 * s_wp
    alpha1 = rz1 / dad1
    alpha0, grow, alpha1 = alpha0[None, :], grow[None, :], alpha1[None, :]
    direction = grow * start_z - alpha0 * scaled_image
    image = grow * first_image - alpha0 * second_image
    solution = alpha0 * start_z + alpha1 * direction
    residual = (start_res - alpha0 * first_image) - alpha1 * image
    both_out = jnp.dot(picks.T, jnp.concatenate([solution, residual], axis=1), precision=exact)
    solution_out = both_out[:, : solution.shape[1]]
    residual_out = both_out[:, solution.shape[1] :]
    return (solution_out[None, None], residual_out[None, None])


def solution(mesh):
    placed = (P("stream", "span", None, None), P("stream", "span", None), P("stream", "span", None))
    return jax.shard_map(
        shards,
        mesh=mesh,
        in_specs=placed,
        out_specs=(P("stream", "span", None, None), P("stream", "span", None, None)),
        check_vma=False,
    )
```

```python
import jax
import jax.numpy as jnp
import numpy as np
from jax import lax
from jax.sharding import PartitionSpec as P

TX = 2
TY = 2
TZ = 24

screening = 0.1
gll_points = [
    -1.0,
    -0.8717401485096066,
    -0.5917001814331423,
    -0.2092992179024789,
    0.0,
    0.2092992179024789,
    0.5917001814331423,
    0.8717401485096066,
    1.0,
]


def legendre_seven(points_in):
    previous = np.ones(points_in.shape)
    current = np.array(points_in)
    for order in range(1, 7):
        following = ((2 * order + 1) * points_in * current - order * previous) / (order + 1)
        previous = current
        current = following
    return current


def gll_tables():
    degree = 7
    gll_nodes = np.array(
        [
            gll_points[0],
            gll_points[1],
            gll_points[2],
            gll_points[3],
            gll_points[5],
            gll_points[6],
            gll_points[7],
            gll_points[8],
        ]
    )
    values = legendre_seven(gll_nodes)
    weights = 2.0 / (degree * (degree + 1) * values**2)
    points = degree + 1
    derivative = np.zeros((points, points))
    mass_matrix = np.zeros((points, points))
    mass_line = weights / 2.0
    for row_index in range(points):
        mass_matrix[row_index, row_index] = mass_line[row_index]
        for col_index in range(points):
            if row_index != col_index:
                derivative[row_index, col_index] = values[row_index] / (
                    values[col_index] * (gll_nodes[row_index] - gll_nodes[col_index])
                )
    derivative[0, 0] = -degree * (degree + 1) / 4.0
    derivative[degree, degree] = degree * (degree + 1) / 4.0
    stiff_line = 2.0 * derivative.T @ (weights[:, None] * derivative)
    stiffness = (
        np.kron(stiff_line, np.kron(mass_matrix, mass_matrix))
        + np.kron(mass_matrix, np.kron(stiff_line, mass_matrix))
        + np.kron(mass_matrix, np.kron(mass_matrix, stiff_line))
    )
    mass_diag = np.kron(mass_line, np.kron(mass_line, mass_line))
    return (stiffness, mass_diag)


def node_weights(tiles_x, tiles_y, tiles_z):
    shared_ends = np.ones(8)
    shared_ends[0] = 2.0
    shared_ends[7] = 2.0
    vertical = np.ones((tiles_z, 8))
    vertical[1:, 0] = 2.0
    vertical[:-1, 7] = 2.0
    total = (
        shared_ends[None, :, None, None]
        * shared_ends[None, None, :, None]
        * vertical[:, None, None, :]
    )
    total = np.broadcast_to(total[None, None], (tiles_x, tiles_y, tiles_z, 8, 8, 8))
    return (1.0 / total).reshape(tiles_x * tiles_y * tiles_z, 512)


def lattice_masks():
    rows = lax.broadcasted_iota(jnp.int32, (TX * TY * TZ, 512), 0)
    lanes = lax.broadcasted_iota(jnp.int32, (TX * TY * TZ, 512), 1)
    layer = rows % TZ
    column = (rows // TZ) % TY
    node_x, node_y, node_z = lanes // 64, (lanes // 8) % 8, lanes % 8
    return {
        "z_up": (node_z == 7) & (layer < TZ - 1),
        "z_down": (node_z == 0) & (layer > 0),
        "x_up": (node_x == 7) & (rows < TY * TZ),
        "x_down": (node_x == 0) & (rows >= TY * TZ),
        "y_up": (node_y == 7) & (column == 0),
        "y_down": (node_y == 0) & (column == 1),
    }


def share_weights():
    rows = lax.broadcasted_iota(jnp.int32, (TX * TY * TZ, 512), 0)
    lanes = lax.broadcasted_iota(jnp.int32, (TX * TY * TZ, 512), 1)
    layer = rows % TZ
    node_x, node_y, node_z = lanes // 64, (lanes // 8) % 8, lanes % 8
    half = jnp.float32(0.5)
    one = jnp.float32(1.0)
    edge_x = jnp.where((node_x == 0) | (node_x == 7), half, one)
    edge_y = jnp.where((node_y == 0) | (node_y == 7), half, one)
    inner_z = ((node_z == 0) & (layer > 0)) | ((node_z == 7) & (layer < TZ - 1))
    edge_z = jnp.where(inner_z, half, one)
    return edge_x * edge_y * edge_z


def shifted(cells, rows, lanes):
    return jnp.roll(jnp.roll(cells, -rows, axis=1), -lanes, axis=2)


def exchange(face, axis, step):
    count = lax.axis_size(axis)
    return lax.ppermute(face, axis, [(i, (i + step) % count) for i in range(count)])


def swap_faces(upper, lower, axis):
    count = lax.axis_size(axis)
    if count % 2:
        return exchange(upper, axis, 1), exchange(lower, axis, -1)
    even = lax.axis_index(axis) % 2 == 0
    inner = [(i, i ^ 1) for i in range(count)]
    outer = [(i, (i + 1) % count if i % 2 else (i - 1) % count) for i in range(count)]
    got_inner = lax.ppermute(jnp.where(even, upper, lower), axis, inner)
    got_outer = lax.ppermute(jnp.where(even, lower, upper), axis, outer)
    return jnp.where(even, got_outer, got_inner), jnp.where(even, got_inner, got_outer)


def face_lanes(plane):
    lanes = lax.broadcasted_iota(jnp.int32, (512, 64), 0)
    slots = lax.broadcasted_iota(jnp.int32, (512, 64), 1)
    return (lanes == (slots // 8) * 64 + plane * 8 + slots % 8).astype(jnp.float32)


def lane_dot(cells, table):
    return jnp.einsum("frn,nc->frc", cells, table, precision=lax.Precision.HIGHEST)


def assemble(stacked):
    masks = lattice_masks()
    zero = jnp.zeros((), stacked.dtype)
    half = TY * TZ
    count = stacked.shape[0]
    cells = stacked
    cells = (
        cells
        + jnp.where(masks["z_up"], shifted(cells, 1, -7), zero)
        + jnp.where(masks["z_down"], shifted(cells, -1, 7), zero)
    )
    upper = cells[:, half:, 448:]
    lower = cells[:, :half, :64]
    from_prev, from_next = swap_faces(upper, lower, "stream")
    inner_x = jnp.where(masks["x_up"], shifted(cells, half, -448), zero) + jnp.where(
        masks["x_down"], shifted(cells, -half, 448), zero
    )
    cells = (
        cells
        + inner_x
        + jnp.pad(from_prev, ((0, 0), (0, half), (0, 448)))
        + jnp.pad(from_next, ((0, 0), (half, 0), (448, 0)))
    )
    blocks = cells.reshape(count, TX, TY, TZ, 512)
    top_lanes = face_lanes(7)
    bottom_lanes = face_lanes(0)
    top = lane_dot(blocks[:, :, 1].reshape(count, TX * TZ, 512), top_lanes)
    bottom = lane_dot(blocks[:, :, 0].reshape(count, TX * TZ, 512), bottom_lanes)
    top_in, bottom_in = swap_faces(top, bottom, "span")
    inner_y = jnp.where(masks["y_up"], shifted(cells, TZ, -56), zero) + jnp.where(
        masks["y_down"], shifted(cells, -TZ, 56), zero
    )
    into_bottom = lane_dot(top_in, bottom_lanes.T).reshape(count, TX, 1, TZ, 512)
    into_top = lane_dot(bottom_in, top_lanes.T).reshape(count, TX, 1, TZ, 512)
    outside = jnp.concatenate([into_bottom, into_top], axis=2).reshape(cells.shape)
    return cells + inner_y + outside


def moved(value, axis, stride, count, shift):
    size = lax.axis_size(axis)
    pairs = []
    for index in range(size):
        spot = (index // stride) % count
        pairs.append((index, index + ((spot + shift) % count - spot) * stride))
    return lax.ppermute(value, axis, pairs)


def group_sum(value, axis, stride, count):
    if count & (count - 1) == 0:
        size = lax.axis_size(axis)
        bit = 1
        while bit < count:
            pairs = [(i, i + ((((i // stride) % count) ^ bit) - (i // stride) % count) * stride) for i in range(size)]
            value = value + lax.ppermute(value, axis, pairs)
            bit *= 2
        return value
    total, width, windows = value, 1, {1: value}
    while width * 2 <= count:
        total = total + moved(total, axis, stride, count, width)
        width *= 2
        windows[width] = total
    rest, shift = count - width, width
    for size in sorted(windows, reverse=True):
        if rest >= size:
            total = total + moved(windows[size], axis, stride, count, shift)
            shift += size
            rest -= size
    return total


def global_sum(value):
    streams = lax.axis_size("stream")
    if streams % 16 == 0:
        groups = ((1, 2), (2, 8), (16, streams // 16))
    else:
        groups = ((1, streams),)
    for stride, count in groups:
        if count > 1:
            value = group_sum(value, "stream", stride, count)
    spans = lax.axis_size("span")
    if spans % 4 == 0 and spans > 4:
        value = group_sum(value, "span", 1, 4)
        return group_sum(value, "span", 4, spans // 4)
    return group_sum(value, "span", 1, spans)


def shards(right_side, conductance, element_slot):
    stiff_np, mass_np = gll_tables()
    stiffness = jnp.asarray(stiff_np, jnp.float32)
    mass_diag = jnp.asarray(mass_np, jnp.float32)
    weights = share_weights()
    slot_index = element_slot[0, 0]
    picks = (slot_index[:, None] == jnp.arange(slot_index.shape[0])[None, :]).astype(jnp.float32)
    exact = lax.Precision.HIGHEST
    forcing = jnp.dot(picks, right_side[0, 0], precision=exact)
    kappa = jnp.dot(picks, conductance[0, 0][:, None], precision=exact)[:, 0]

    def local_dot(first_vec, second_vec):
        return jnp.sum(first_vec * second_vec * weights)

    def apply_local(field):
        return (
            kappa[:, None] * jnp.dot(field, stiffness, precision=lax.Precision.HIGHEST)
            + screening * mass_diag[None, :] * field
        )

    stiff_diag = jnp.asarray(np.diag(stiff_np), jnp.float32)
    diag_local = kappa[:, None] * stiff_diag[None, :] + screening * mass_diag[None, :]
    both = assemble(jnp.stack([mass_diag[None, :] * forcing, diag_local]))
    start_res = both[0]
    diag_field = both[1]
    start_z = start_res / diag_field
    first_local = apply_local(start_z)
    first_image = assemble(first_local[None])[0]
    scaled_image = first_image / diag_field
    second_local = apply_local(scaled_image)
    lane_sums = jnp.stack(
        [
            jnp.sum(start_res * start_z * weights, axis=0),
            jnp.sum(start_z * first_local, axis=0),
            jnp.sum(start_res * scaled_image * weights, axis=0),
            jnp.sum(first_image * scaled_image * weights, axis=0),
            jnp.sum(start_z * second_local, axis=0),
            jnp.sum(scaled_image * second_local, axis=0),
        ]
    )
    span = lane_sums.shape[1] // 2
    while span >= 1:
        lane_sums = lane_sums + jnp.roll(lane_sums, span, axis=1)
        span //= 2
    sums = global_sum(lane_sums)
    second_image = assemble(second_local[None])[0]
    s_rz, s_zq, s_rw, s_qw, s_zp, s_wp = (sums[n] for n in range(6))
    alpha0 = s_rz / s_zq
    rz1 = s_rz - alpha0 * (s_rw + s_zq) + alpha0 * alpha0 * s_qw
    beta = rz1 / s_rz
    grow = 1.0 + beta
    dad1 = grow * grow * s_zq - alpha0 * grow * (s_zp + s_qw) + alpha0 * alpha0 * s_wp
    alpha1 = rz1 / dad1
    alpha0, grow, alpha1 = alpha0[None, :], grow[None, :], alpha1[None, :]
    direction = grow * start_z - alpha0 * scaled_image
    image = grow * first_image - alpha0 * second_image
    solution = alpha0 * start_z + alpha1 * direction
    residual = (start_res - alpha0 * first_image) - alpha1 * image
    both_out = jnp.dot(picks.T, jnp.concatenate([solution, residual], axis=1), precision=exact)
    solution_out = both_out[:, : solution.shape[1]]
    residual_out = both_out[:, solution.shape[1] :]
    return (solution_out[None, None], residual_out[None, None])


def solution(mesh):
    placed = (P("stream", "span", None, None), P("stream", "span", None), P("stream", "span", None))
    return jax.shard_map(
        shards,
        mesh=mesh,
        in_specs=placed,
        out_specs=(P("stream", "span", None, None), P("stream", "span", None, None)),
        check_vma=False,
    )
```

```python
import jax
import jax.numpy as jnp
import numpy as np
from jax import lax
from jax.sharding import PartitionSpec as P

TX = 2
TY = 2
TZ = 24

screening = 0.1
gll_points = [
    -1.0,
    -0.8717401485096066,
    -0.5917001814331423,
    -0.2092992179024789,
    0.0,
    0.2092992179024789,
    0.5917001814331423,
    0.8717401485096066,
    1.0,
]


def legendre_seven(points_in):
    previous = np.ones(points_in.shape)
    current = np.array(points_in)
    for order in range(1, 7):
        following = ((2 * order + 1) * points_in * current - order * previous) / (order + 1)
        previous = current
        current = following
    return current


def gll_tables():
    degree = 7
    gll_nodes = np.array(
        [
            gll_points[0],
            gll_points[1],
            gll_points[2],
            gll_points[3],
            gll_points[5],
            gll_points[6],
            gll_points[7],
            gll_points[8],
        ]
    )
    values = legendre_seven(gll_nodes)
    weights = 2.0 / (degree * (degree + 1) * values**2)
    points = degree + 1
    derivative = np.zeros((points, points))
    mass_matrix = np.zeros((points, points))
    mass_line = weights / 2.0
    for row_index in range(points):
        mass_matrix[row_index, row_index] = mass_line[row_index]
        for col_index in range(points):
            if row_index != col_index:
                derivative[row_index, col_index] = values[row_index] / (
                    values[col_index] * (gll_nodes[row_index] - gll_nodes[col_index])
                )
    derivative[0, 0] = -degree * (degree + 1) / 4.0
    derivative[degree, degree] = degree * (degree + 1) / 4.0
    stiff_line = 2.0 * derivative.T @ (weights[:, None] * derivative)
    stiffness = (
        np.kron(stiff_line, np.kron(mass_matrix, mass_matrix))
        + np.kron(mass_matrix, np.kron(stiff_line, mass_matrix))
        + np.kron(mass_matrix, np.kron(mass_matrix, stiff_line))
    )
    mass_diag = np.kron(mass_line, np.kron(mass_line, mass_line))
    return (stiffness, mass_diag)


def node_weights(tiles_x, tiles_y, tiles_z):
    shared_ends = np.ones(8)
    shared_ends[0] = 2.0
    shared_ends[7] = 2.0
    vertical = np.ones((tiles_z, 8))
    vertical[1:, 0] = 2.0
    vertical[:-1, 7] = 2.0
    total = (
        shared_ends[None, :, None, None]
        * shared_ends[None, None, :, None]
        * vertical[:, None, None, :]
    )
    total = np.broadcast_to(total[None, None], (tiles_x, tiles_y, tiles_z, 8, 8, 8))
    return (1.0 / total).reshape(tiles_x * tiles_y * tiles_z, 512)


def lattice_masks():
    rows = lax.broadcasted_iota(jnp.int32, (TX * TY * TZ, 512), 0)
    lanes = lax.broadcasted_iota(jnp.int32, (TX * TY * TZ, 512), 1)
    layer = rows % TZ
    column = (rows // TZ) % TY
    node_x, node_y, node_z = lanes // 64, (lanes // 8) % 8, lanes % 8
    return {
        "z_up": (node_z == 7) & (layer < TZ - 1),
        "z_down": (node_z == 0) & (layer > 0),
        "x_up": (node_x == 7) & (rows < TY * TZ),
        "x_down": (node_x == 0) & (rows >= TY * TZ),
        "y_up": (node_y == 7) & (column == 0),
        "y_down": (node_y == 0) & (column == 1),
    }


def share_weights():
    rows = lax.broadcasted_iota(jnp.int32, (TX * TY * TZ, 512), 0)
    lanes = lax.broadcasted_iota(jnp.int32, (TX * TY * TZ, 512), 1)
    layer = rows % TZ
    node_x, node_y, node_z = lanes // 64, (lanes // 8) % 8, lanes % 8
    half = jnp.float32(0.5)
    one = jnp.float32(1.0)
    edge_x = jnp.where((node_x == 0) | (node_x == 7), half, one)
    edge_y = jnp.where((node_y == 0) | (node_y == 7), half, one)
    inner_z = ((node_z == 0) & (layer > 0)) | ((node_z == 7) & (layer < TZ - 1))
    edge_z = jnp.where(inner_z, half, one)
    return edge_x * edge_y * edge_z


def shifted(cells, rows, lanes):
    return jnp.roll(jnp.roll(cells, -rows, axis=1), -lanes, axis=2)


def exchange(face, axis, step):
    count = lax.axis_size(axis)
    return lax.ppermute(face, axis, [(i, (i + step) % count) for i in range(count)])


def swap_faces(upper, lower, axis, extra=None):
    count = lax.axis_size(axis)
    if count % 2:
        return exchange(upper, axis, 1), exchange(lower, axis, -1), None
    even = lax.axis_index(axis) % 2 == 0
    inner = [(i, i ^ 1) for i in range(count)]
    outer = [(i, (i + 1) % count if i % 2 else (i - 1) % count) for i in range(count)]
    sent = jnp.where(even, upper, lower)
    if extra is not None:
        sent = jnp.concatenate([sent, extra.reshape((1,) + sent.shape[1:])], axis=0)
    got_inner = lax.ppermute(sent, axis, inner)
    got_extra = None
    if extra is not None:
        got_extra = got_inner[1:].reshape(extra.shape)
        got_inner = got_inner[:1]
    got_outer = lax.ppermute(jnp.where(even, lower, upper), axis, outer)
    return jnp.where(even, got_outer, got_inner), jnp.where(even, got_inner, got_outer), got_extra


def face_lanes(plane):
    lanes = lax.broadcasted_iota(jnp.int32, (512, 64), 0)
    slots = lax.broadcasted_iota(jnp.int32, (512, 64), 1)
    return (lanes == (slots // 8) * 64 + plane * 8 + slots % 8).astype(jnp.float32)


def lane_dot(cells, table):
    return jnp.einsum("frn,nc->frc", cells, table, precision=lax.Precision.HIGHEST)


def assemble(stacked, extra=None):
    masks = lattice_masks()
    zero = jnp.zeros((), stacked.dtype)
    half = TY * TZ
    count = stacked.shape[0]
    cells = stacked
    cells = (
        cells
        + jnp.where(masks["z_up"], shifted(cells, 1, -7), zero)
        + jnp.where(masks["z_down"], shifted(cells, -1, 7), zero)
    )
    upper = cells[:, half:, 448:]
    lower = cells[:, :half, :64]
    from_prev, from_next, got_extra = swap_faces(upper, lower, "stream", extra)
    inner_x = jnp.where(masks["x_up"], shifted(cells, half, -448), zero) + jnp.where(
        masks["x_down"], shifted(cells, -half, 448), zero
    )
    cells = (
        cells
        + inner_x
        + jnp.pad(from_prev, ((0, 0), (0, half), (0, 448)))
        + jnp.pad(from_next, ((0, 0), (half, 0), (448, 0)))
    )
    blocks = cells.reshape(count, TX, TY, TZ, 512)
    top_lanes = face_lanes(7)
    bottom_lanes = face_lanes(0)
    top = lane_dot(blocks[:, :, 1].reshape(count, TX * TZ, 512), top_lanes)
    bottom = lane_dot(blocks[:, :, 0].reshape(count, TX * TZ, 512), bottom_lanes)
    top_in, bottom_in, _ = swap_faces(top, bottom, "span")
    inner_y = jnp.where(masks["y_up"], shifted(cells, TZ, -56), zero) + jnp.where(
        masks["y_down"], shifted(cells, -TZ, 56), zero
    )
    into_bottom = lane_dot(top_in, bottom_lanes.T).reshape(count, TX, 1, TZ, 512)
    into_top = lane_dot(bottom_in, top_lanes.T).reshape(count, TX, 1, TZ, 512)
    outside = jnp.concatenate([into_bottom, into_top], axis=2).reshape(cells.shape)
    if extra is None:
        return cells + inner_y + outside
    return cells + inner_y + outside, got_extra


def moved(value, axis, stride, count, shift):
    size = lax.axis_size(axis)
    pairs = []
    for index in range(size):
        spot = (index // stride) % count
        pairs.append((index, index + ((spot + shift) % count - spot) * stride))
    return lax.ppermute(value, axis, pairs)


def group_sum(value, axis, stride, count):
    if count & (count - 1) == 0:
        size = lax.axis_size(axis)
        bit = 1
        while bit < count:
            pairs = [(i, i + ((((i // stride) % count) ^ bit) - (i // stride) % count) * stride) for i in range(size)]
            value = value + lax.ppermute(value, axis, pairs)
            bit *= 2
        return value
    total, width, windows = value, 1, {1: value}
    while width * 2 <= count:
        total = total + moved(total, axis, stride, count, width)
        width *= 2
        windows[width] = total
    rest, shift = count - width, width
    for size in sorted(windows, reverse=True):
        if rest >= size:
            total = total + moved(windows[size], axis, stride, count, shift)
            shift += size
            rest -= size
    return total


def global_sum(value, core_done=False):
    streams = lax.axis_size("stream")
    if core_done:
        groups = ((2, 8), (16, streams // 16)) if streams % 16 == 0 else ((2, streams // 2),)
    elif streams % 16 == 0:
        groups = ((1, 2), (2, 8), (16, streams // 16))
    else:
        groups = ((1, streams),)
    for stride, count in groups:
        if count > 1:
            value = group_sum(value, "stream", stride, count)
    spans = lax.axis_size("span")
    if spans % 4 == 0 and spans > 4:
        value = group_sum(value, "span", 1, 4)
        return group_sum(value, "span", 4, spans // 4)
    return group_sum(value, "span", 1, spans)


def shards(right_side, conductance, element_slot):
    stiff_np, mass_np = gll_tables()
    stiffness = jnp.asarray(stiff_np, jnp.float32)
    mass_diag = jnp.asarray(mass_np, jnp.float32)
    weights = share_weights()
    slot_index = element_slot[0, 0]
    picks = (slot_index[:, None] == jnp.arange(slot_index.shape[0])[None, :]).astype(jnp.float32)
    exact = lax.Precision.HIGHEST
    forcing = jnp.dot(picks, right_side[0, 0], precision=exact)
    kappa = jnp.dot(picks, conductance[0, 0][:, None], precision=exact)[:, 0]

    def local_dot(first_vec, second_vec):
        return jnp.sum(first_vec * second_vec * weights)

    def apply_local(field):
        return (
            kappa[:, None] * jnp.dot(field, stiffness, precision=lax.Precision.HIGHEST)
            + screening * mass_diag[None, :] * field
        )

    stiff_diag = jnp.asarray(np.diag(stiff_np), jnp.float32)
    diag_local = kappa[:, None] * stiff_diag[None, :] + screening * mass_diag[None, :]
    both = assemble(jnp.stack([mass_diag[None, :] * forcing, diag_local]))
    start_res = both[0]
    diag_field = both[1]
    start_z = start_res / diag_field
    first_local = apply_local(start_z)
    first_image = assemble(first_local[None])[0]
    scaled_image = first_image / diag_field
    second_local = apply_local(scaled_image)
    lane_sums = jnp.stack(
        [
            jnp.sum(start_res * start_z * weights, axis=0),
            jnp.sum(start_z * first_local, axis=0),
            jnp.sum(start_res * scaled_image * weights, axis=0),
            jnp.sum(first_image * scaled_image * weights, axis=0),
            jnp.sum(start_z * second_local, axis=0),
            jnp.sum(scaled_image * second_local, axis=0),
        ]
    )
    span = lane_sums.shape[1] // 2
    while span >= 1:
        lane_sums = lane_sums + jnp.roll(lane_sums, span, axis=1)
        span //= 2
    if lax.axis_size("stream") % 2 == 0:
        second_image, partner = assemble(second_local[None], lane_sums)
        sums = global_sum(lane_sums + partner, core_done=True)
    else:
        second_image = assemble(second_local[None])
        sums = global_sum(lane_sums)
    second_image = second_image[0]
    s_rz, s_zq, s_rw, s_qw, s_zp, s_wp = (sums[n] for n in range(6))
    alpha0 = s_rz / s_zq
    rz1 = s_rz - alpha0 * (s_rw + s_zq) + alpha0 * alpha0 * s_qw
    beta = rz1 / s_rz
    grow = 1.0 + beta
    dad1 = grow * grow * s_zq - alpha0 * grow * (s_zp + s_qw) + alpha0 * alpha0 * s_wp
    alpha1 = rz1 / dad1
    alpha0, grow, alpha1 = alpha0[None, :], grow[None, :], alpha1[None, :]
    direction = grow * start_z - alpha0 * scaled_image
    image = grow * first_image - alpha0 * second_image
    solution = alpha0 * start_z + alpha1 * direction
    residual = (start_res - alpha0 * first_image) - alpha1 * image
    both_out = jnp.dot(picks.T, jnp.concatenate([solution, residual], axis=1), precision=exact)
    solution_out = both_out[:, : solution.shape[1]]
    residual_out = both_out[:, solution.shape[1] :]
    return (solution_out[None, None], residual_out[None, None])


def solution(mesh):
    placed = (P("stream", "span", None, None), P("stream", "span", None), P("stream", "span", None))
    return jax.shard_map(
        shards,
        mesh=mesh,
        in_specs=placed,
        out_specs=(P("stream", "span", None, None), P("stream", "span", None, None)),
        check_vma=False,
    )
```

```python
import jax
import jax.numpy as jnp
import numpy as np
from jax import lax
from jax.sharding import PartitionSpec as P

TX = 2
TY = 2
TZ = 24

screening = 0.1
gll_points = [
    -1.0,
    -0.8717401485096066,
    -0.5917001814331423,
    -0.2092992179024789,
    0.0,
    0.2092992179024789,
    0.5917001814331423,
    0.8717401485096066,
    1.0,
]


def legendre_seven(points_in):
    previous = np.ones(points_in.shape)
    current = np.array(points_in)
    for order in range(1, 7):
        following = ((2 * order + 1) * points_in * current - order * previous) / (order + 1)
        previous = current
        current = following
    return current


def gll_tables():
    degree = 7
    gll_nodes = np.array(
        [
            gll_points[0],
            gll_points[1],
            gll_points[2],
            gll_points[3],
            gll_points[5],
            gll_points[6],
            gll_points[7],
            gll_points[8],
        ]
    )
    values = legendre_seven(gll_nodes)
    weights = 2.0 / (degree * (degree + 1) * values**2)
    points = degree + 1
    derivative = np.zeros((points, points))
    mass_matrix = np.zeros((points, points))
    mass_line = weights / 2.0
    for row_index in range(points):
        mass_matrix[row_index, row_index] = mass_line[row_index]
        for col_index in range(points):
            if row_index != col_index:
                derivative[row_index, col_index] = values[row_index] / (
                    values[col_index] * (gll_nodes[row_index] - gll_nodes[col_index])
                )
    derivative[0, 0] = -degree * (degree + 1) / 4.0
    derivative[degree, degree] = degree * (degree + 1) / 4.0
    stiff_line = 2.0 * derivative.T @ (weights[:, None] * derivative)
    stiffness = (
        np.kron(stiff_line, np.kron(mass_matrix, mass_matrix))
        + np.kron(mass_matrix, np.kron(stiff_line, mass_matrix))
        + np.kron(mass_matrix, np.kron(mass_matrix, stiff_line))
    )
    mass_diag = np.kron(mass_line, np.kron(mass_line, mass_line))
    return (stiffness, mass_diag)


def node_weights(tiles_x, tiles_y, tiles_z):
    shared_ends = np.ones(8)
    shared_ends[0] = 2.0
    shared_ends[7] = 2.0
    vertical = np.ones((tiles_z, 8))
    vertical[1:, 0] = 2.0
    vertical[:-1, 7] = 2.0
    total = (
        shared_ends[None, :, None, None]
        * shared_ends[None, None, :, None]
        * vertical[:, None, None, :]
    )
    total = np.broadcast_to(total[None, None], (tiles_x, tiles_y, tiles_z, 8, 8, 8))
    return (1.0 / total).reshape(tiles_x * tiles_y * tiles_z, 512)


def lattice_masks():
    rows = lax.broadcasted_iota(jnp.int32, (TX * TY * TZ, 512), 0)
    lanes = lax.broadcasted_iota(jnp.int32, (TX * TY * TZ, 512), 1)
    layer = rows % TZ
    column = (rows // TZ) % TY
    node_x, node_y, node_z = lanes // 64, (lanes // 8) % 8, lanes % 8
    return {
        "z_up": (node_z == 7) & (layer < TZ - 1),
        "z_down": (node_z == 0) & (layer > 0),
        "x_up": (node_x == 7) & (rows < TY * TZ),
        "x_down": (node_x == 0) & (rows >= TY * TZ),
        "y_up": (node_y == 7) & (column == 0),
        "y_down": (node_y == 0) & (column == 1),
    }


def share_weights():
    rows = lax.broadcasted_iota(jnp.int32, (TX * TY * TZ, 512), 0)
    lanes = lax.broadcasted_iota(jnp.int32, (TX * TY * TZ, 512), 1)
    layer = rows % TZ
    node_x, node_y, node_z = lanes // 64, (lanes // 8) % 8, lanes % 8
    half = jnp.float32(0.5)
    one = jnp.float32(1.0)
    edge_x = jnp.where((node_x == 0) | (node_x == 7), half, one)
    edge_y = jnp.where((node_y == 0) | (node_y == 7), half, one)
    inner_z = ((node_z == 0) & (layer > 0)) | ((node_z == 7) & (layer < TZ - 1))
    edge_z = jnp.where(inner_z, half, one)
    return edge_x * edge_y * edge_z


def shifted(cells, rows, lanes):
    return jnp.roll(jnp.roll(cells, -rows, axis=1), -lanes, axis=2)


def exchange(face, axis, step):
    count = lax.axis_size(axis)
    return lax.ppermute(face, axis, [(i, (i + step) % count) for i in range(count)])


def swap_faces(upper, lower, axis):
    count = lax.axis_size(axis)
    if count % 2:
        return exchange(upper, axis, 1), exchange(lower, axis, -1)
    even = lax.axis_index(axis) % 2 == 0
    inner = [(i, i ^ 1) for i in range(count)]
    outer = [(i, (i + 1) % count if i % 2 else (i - 1) % count) for i in range(count)]
    got_inner = lax.ppermute(jnp.where(even, upper, lower), axis, inner)
    got_outer = lax.ppermute(jnp.where(even, lower, upper), axis, outer)
    return jnp.where(even, got_outer, got_inner), jnp.where(even, got_inner, got_outer)


def face_lanes(plane):
    lanes = lax.broadcasted_iota(jnp.int32, (512, 64), 0)
    slots = lax.broadcasted_iota(jnp.int32, (512, 64), 1)
    return (lanes == (slots // 8) * 64 + plane * 8 + slots % 8).astype(jnp.float32)


def lane_dot(cells, table):
    return jnp.einsum("frn,nc->frc", cells, table, precision=lax.Precision.HIGHEST)


def assemble(stacked):
    masks = lattice_masks()
    zero = jnp.zeros((), stacked.dtype)
    half = TY * TZ
    count = stacked.shape[0]
    cells = stacked
    cells = (
        cells
        + jnp.where(masks["z_up"], shifted(cells, 1, -7), zero)
        + jnp.where(masks["z_down"], shifted(cells, -1, 7), zero)
    )
    upper = cells[:, half:, 448:]
    lower = cells[:, :half, :64]
    from_prev, from_next = swap_faces(upper, lower, "stream")
    inner_x = jnp.where(masks["x_up"], shifted(cells, half, -448), zero) + jnp.where(
        masks["x_down"], shifted(cells, -half, 448), zero
    )
    cells = (
        cells
        + inner_x
        + jnp.pad(from_prev, ((0, 0), (0, half), (0, 448)))
        + jnp.pad(from_next, ((0, 0), (half, 0), (448, 0)))
    )
    blocks = cells.reshape(count, TX, TY, TZ, 512)
    top_lanes = face_lanes(7)
    bottom_lanes = face_lanes(0)
    top = lane_dot(blocks[:, :, 1].reshape(count, TX * TZ, 512), top_lanes)
    bottom = lane_dot(blocks[:, :, 0].reshape(count, TX * TZ, 512), bottom_lanes)
    top_in, bottom_in = swap_faces(top, bottom, "span")
    inner_y = jnp.where(masks["y_up"], shifted(cells, TZ, -56), zero) + jnp.where(
        masks["y_down"], shifted(cells, -TZ, 56), zero
    )
    into_bottom = lane_dot(top_in, bottom_lanes.T).reshape(count, TX, 1, TZ, 512)
    into_top = lane_dot(bottom_in, top_lanes.T).reshape(count, TX, 1, TZ, 512)
    outside = jnp.concatenate([into_bottom, into_top], axis=2).reshape(cells.shape)
    return cells + inner_y + outside


def moved(value, axis, stride, count, shift):
    size = lax.axis_size(axis)
    pairs = []
    for index in range(size):
        spot = (index // stride) % count
        pairs.append((index, index + ((spot + shift) % count - spot) * stride))
    return lax.ppermute(value, axis, pairs)


def group_sum(value, axis, stride, count):
    if count & (count - 1) == 0:
        size = lax.axis_size(axis)
        bit = 1
        while bit < count:
            pairs = [(i, i + ((((i // stride) % count) ^ bit) - (i // stride) % count) * stride) for i in range(size)]
            value = value + lax.ppermute(value, axis, pairs)
            bit *= 2
        return value
    total, width, windows = value, 1, {1: value}
    while width * 2 <= count:
        total = total + moved(total, axis, stride, count, width)
        width *= 2
        windows[width] = total
    rest, shift = count - width, width
    for size in sorted(windows, reverse=True):
        if rest >= size:
            total = total + moved(windows[size], axis, stride, count, shift)
            shift += size
            rest -= size
    return total


def global_sum(value):
    spans = lax.axis_size("span")
    if spans % 4 == 0 and spans > 4:
        value = group_sum(value, "span", 4, spans // 4)
        value = group_sum(value, "span", 1, 4)
    else:
        value = group_sum(value, "span", 1, spans)
    streams = lax.axis_size("stream")
    if streams % 16 == 0:
        groups = ((1, 2), (2, 8), (16, streams // 16))
    else:
        groups = ((1, streams),)
    for stride, count in groups:
        if count > 1:
            value = group_sum(value, "stream", stride, count)
    return value


def shards(right_side, conductance, element_slot):
    stiff_np, mass_np = gll_tables()
    stiffness = jnp.asarray(stiff_np, jnp.float32)
    mass_diag = jnp.asarray(mass_np, jnp.float32)
    weights = share_weights()
    slot_index = element_slot[0, 0]
    picks = (slot_index[:, None] == jnp.arange(slot_index.shape[0])[None, :]).astype(jnp.float32)
    exact = lax.Precision.HIGHEST
    forcing = jnp.dot(picks, right_side[0, 0], precision=exact)
    kappa = jnp.dot(picks, conductance[0, 0][:, None], precision=exact)[:, 0]

    def local_dot(first_vec, second_vec):
        return jnp.sum(first_vec * second_vec * weights)

    def apply_local(field):
        return (
            kappa[:, None] * jnp.dot(field, stiffness, precision=lax.Precision.HIGHEST)
            + screening * mass_diag[None, :] * field
        )

    stiff_diag = jnp.asarray(np.diag(stiff_np), jnp.float32)
    diag_local = kappa[:, None] * stiff_diag[None, :] + screening * mass_diag[None, :]
    both = assemble(jnp.stack([mass_diag[None, :] * forcing, diag_local]))
    start_res = both[0]
    diag_field = both[1]
    start_z = start_res / diag_field
    first_local = apply_local(start_z)
    first_image = assemble(first_local[None])[0]
    scaled_image = first_image / diag_field
    second_local = apply_local(scaled_image)
    lane_sums = jnp.stack(
        [
            jnp.sum(start_res * start_z * weights, axis=0),
            jnp.sum(start_z * first_local, axis=0),
            jnp.sum(start_res * scaled_image * weights, axis=0),
            jnp.sum(first_image * scaled_image * weights, axis=0),
            jnp.sum(start_z * second_local, axis=0),
            jnp.sum(scaled_image * second_local, axis=0),
        ]
    )
    span = lane_sums.shape[1] // 2
    while span >= 1:
        lane_sums = lane_sums + jnp.roll(lane_sums, span, axis=1)
        span //= 2
    sums = global_sum(lane_sums)
    second_image = assemble(second_local[None])[0]
    s_rz, s_zq, s_rw, s_qw, s_zp, s_wp = (sums[n] for n in range(6))
    alpha0 = s_rz / s_zq
    rz1 = s_rz - alpha0 * (s_rw + s_zq) + alpha0 * alpha0 * s_qw
    beta = rz1 / s_rz
    grow = 1.0 + beta
    dad1 = grow * grow * s_zq - alpha0 * grow * (s_zp + s_qw) + alpha0 * alpha0 * s_wp
    alpha1 = rz1 / dad1
    alpha0, grow, alpha1 = alpha0[None, :], grow[None, :], alpha1[None, :]
    direction = grow * start_z - alpha0 * scaled_image
    image = grow * first_image - alpha0 * second_image
    solution = alpha0 * start_z + alpha1 * direction
    residual = (start_res - alpha0 * first_image) - alpha1 * image
    both_out = jnp.dot(picks.T, jnp.concatenate([solution, residual], axis=1), precision=exact)
    solution_out = both_out[:, : solution.shape[1]]
    residual_out = both_out[:, solution.shape[1] :]
    return (solution_out[None, None], residual_out[None, None])


def solution(mesh):
    placed = (P("stream", "span", None, None), P("stream", "span", None), P("stream", "span", None))
    return jax.shard_map(
        shards,
        mesh=mesh,
        in_specs=placed,
        out_specs=(P("stream", "span", None, None), P("stream", "span", None, None)),
        check_vma=False,
    )
```
